32 devices in a mesh: groups: 2 (over x), blk: 16 (over z, y, core).
Axes of the slice: x: 2, y: 2, z: 4, core: 2. Of those that a mesh axis runs over, the one named last changes fastest.
Arguments:
- layer_input_tokens: bfloat16 [384, 8192], P('groups', 'blk'), parts along dimension 0, may hold values from -6 to 6
- input_norm_gain: float32 [8192], replicated, may hold values from 0.5 to 1.5
- query_weight: bfloat16 [8192, 8192], P(None, 'blk'), may hold values from -0.0625 to 0.0625
- key_value_weight: bfloat16 [8192, 2048], P(None, 'blk'), may hold values from -0.0625 to 0.0625
- output_weight: bfloat16 [8192, 8192], P(None, 'blk'), may hold values from -0.5 to 0.5
- adapter_down_weight: bfloat16 [16, 64, 8192], P('blk'), may hold values from -0.0625 to 0.0625
- adapter_up_weight: bfloat16 [16, 64, 8192], P(None, None, 'blk'), may hold values from -0.75 to 0.75
- key_value_page_pool: bfloat16 [512, 128, 2048], P(('groups', 'blk')), parts along dimension 0, may hold values from -240 to 240
- request_adapter: int32 [128], P('groups'), parts along dimension 0, may hold values from 0 to 15
- adapter_storage_slot: int32 [16], replicated, may hold values from 0 to 15, each once
- cached_lengths: int32 [128], P('groups'), parts along dimension 0, may hold values from 1 to 512, as said below
- request_page_tables: int32 [128, 4], P('groups'), parts along dimension 0, may hold values from -1 to 255, as said below
Outputs:
- layer_out: bfloat16 [384, 8192], P('groups', 'blk'), parts along dimension 0
The draws below stay inside these ranges and needn't reach their ends.
There are 2 independent parts, one for each index of `groups`. The reference program is written for one: setup_inputs(seed, part) draws one part's arguments, and reference() takes and returns one part's arrays. A program takes and returns all parts, laid end to end along the dimension named above; an argument that names none is the same for every part. Nothing has to cross between parts.
Inputs may be any that keep to these rules, and one draw needn't show every extreme that they name: `cached_lengths`: each request's cached length; the longest is exactly 512. `request_page_tables`: row r holds ceil(cached_lengths[r] / 128) page numbers first and -1 after them; no page is named twice in the whole table.
All inputs are finite; a program needn't handle non-finite values.
Results may differ from the reference program's by a relative error of at most 0.0085.
The reference program's roundings to bfloat16 on the way count: a program that leaves them out, or rounds other values in their place, can miss the bound.
Values may be sent and summed in bfloat16 or wider, within the bound.
No kernel may reach another device: no remote copies, remote signals or barrier semaphores. Data moves between devices by JAX's collectives and lax.ppermute only.
A program may use at most 128 MiB of HBM per device.

```python
import math
import jax
import jax.numpy as jnp
import numpy as np
from jax import lax

MODEL_WIDTH = 8192
QUERY_HEADS = 64
KEY_VALUE_HEADS = 8
HEAD_WIDTH = 128
ADAPTER_RANK = 64
PAGE_LENGTH = 128
NEW_TOKENS = 3
REQS = 64
QUERY_WIDTH = 8192
KVW = 2048
TOKENS = 192
PAGES = 256
MAXP = 4
ADAPTER_COUNT = 16


def draw_tables_common(key):
    folded = jax.random.fold_in(key, 17)
    key_len, key_long, key_perm = jax.random.split(folded, 3)
    lengths = jax.random.randint(key_len, (REQS,), 1, MAXP * PAGE_LENGTH + 1)
    longest = jax.random.randint(key_long, (), 0, REQS)
    shorter = (longest + 1) % REQS
    request_ids = jnp.arange(REQS)
    lengths = jnp.where(request_ids == shorter, jnp.minimum(lengths, (MAXP - 1) * PAGE_LENGTH), lengths)
    lengths = jnp.where(request_ids == longest, MAXP * PAGE_LENGTH, lengths).astype(jnp.int32)
    page_order = jax.random.permutation(key_perm, PAGES).astype(jnp.int32)
    page_ids = jnp.arange(PAGES, dtype=jnp.int32)
    top_place = jnp.sum(jnp.where(page_order == PAGES - 1, page_ids, 0))
    target_place = longest * MAXP
    target_value = jnp.sum(jnp.where(page_ids == target_place, page_order, 0))
    page_order = jnp.where(page_ids == top_place, target_value, page_order)
    page_order = jnp.where(page_ids == target_place, PAGES - 1, page_order).astype(jnp.int32)
    used_pages = (lengths + PAGE_LENGTH - 1) // PAGE_LENGTH
    page_grid = page_order.reshape(REQS, MAXP)
    tables = jnp.where(jnp.arange(MAXP)[None, :] < used_pages[:, None], page_grid, -1).astype(jnp.int32)
    return (lengths, tables)


def draw_cached_lengths(key, part):
    return draw_tables_common(key)[0]


def draw_request_page_tables(key, part):
    return draw_tables_common(key)[1]


def draw_key_value_page_pool(key, part):
    folded = jax.random.fold_in(key, 29)
    key_val = jax.random.fold_in(folded, 0)
    values = jax.random.truncated_normal(key_val, -6.0, 6.0, (PAGES, PAGE_LENGTH, KVW), jnp.float32)
    return values.astype(jnp.bfloat16)


def touch_ends(array, stream_key, smallest, top_value):
    place = [jax.random.randint(jax.random.fold_in(stream_key, axis), (), 0, length) for axis, length in enumerate(array.shape)]
    widest = array.shape.index(max(array.shape))
    next_to = place[:widest] + [(place[widest] + 1) % array.shape[widest]] + place[widest + 1:]
    return array.at[tuple(place)].set(smallest).at[tuple(next_to)].set(top_value)


def shard_levels(own_key, dims, cuts, low, top_value):
    loudness, own = 1.0, jax.random.fold_in(own_key, 6)
    for axis_at, blocks in cuts:
        draws = jnp.exp(jax.random.uniform(jax.random.fold_in(own, axis_at), (blocks,), jnp.float32, low / len(cuts), top_value / len(cuts)))
        loudness = loudness * jnp.repeat(draws, dims[axis_at] // blocks).reshape([-1 if axis == axis_at else 1 for axis in range(len(dims))])
    return loudness


def cumulative_ranks(number_of, lean):
    portions = [(1 << 20) // math.isqrt(standing ** lean) + 1 for standing in range(1, number_of + 1)]
    width = 1 + sum(portions) // (1 << 30)
    return np.cumsum(np.array([max(1, weight // width) for weight in portions]))


def ranked(stream_key, extent, number_of, skew):
    listing = cumulative_ranks(number_of, skew)
    ticket = jax.random.randint(jax.random.fold_in(stream_key, 1), extent, 0, int(listing[number_of - 1]))
    grade = jnp.searchsorted(jnp.asarray(listing, jnp.int32), ticket, side="right")
    return jax.random.permutation(jax.random.fold_in(stream_key, 2), number_of)[grade].astype(jnp.int32)


def normal_values(rng, extent, spread, most, shards=(), held_as=jnp.bfloat16):
    values = jax.random.normal(rng, extent, jnp.float32) * spread
    if len(shards) > 0:
        values = shard_levels(rng, extent, shards, -0.22, 0.18) * values
    return jnp.clip(values, min=-most, max=most).astype(held_as)


def setup_inputs(seed: int = 0, part: int = 0) -> dict:
    key_list = jax.random.split(jax.random.key(seed), 13)
    part_splits = jax.random.split(jax.random.fold_in(key_list[12], part), 13)
    return {
        "layer_input_tokens": normal_values(part_splits[0], (TOKENS, MODEL_WIDTH), 1.0, 6.0, ((1, 16),)),
        "input_norm_gain": jnp.clip(1.0 + 0.1 * jax.random.normal(key_list[1], (MODEL_WIDTH,), jnp.float32), 0.5, 1.5),
        "query_weight": normal_values(key_list[2], (MODEL_WIDTH, QUERY_WIDTH), MODEL_WIDTH ** -0.5, 0.0625, ((1, 16),)),
        "key_value_weight": normal_values(key_list[3], (MODEL_WIDTH, KVW), MODEL_WIDTH ** -0.5, 0.0625, ((1, 16),)),
        "output_weight": normal_values(key_list[4], (QUERY_WIDTH, MODEL_WIDTH), HEAD_WIDTH ** -0.5, 0.5, ((1, 16),)),
        "adapter_down_weight": normal_values(key_list[5], (ADAPTER_COUNT, ADAPTER_RANK, MODEL_WIDTH), MODEL_WIDTH ** -0.5, 0.0625, ((0, 16),)),
        "adapter_up_weight": normal_values(key_list[6], (ADAPTER_COUNT, ADAPTER_RANK, QUERY_WIDTH), ADAPTER_RANK ** -0.5, 0.75, ((2, 16),)),
        "key_value_page_pool": draw_key_value_page_pool(jax.random.fold_in(jax.random.fold_in(key_list[12], part), 71), part),
        "request_adapter": touch_ends(ranked(part_splits[8], (REQS,), ADAPTER_COUNT, 2), jax.random.fold_in(part_splits[8], 3), 0, ADAPTER_COUNT - 1).astype(jnp.int32),
        "adapter_storage_slot": jax.random.permutation(key_list[9], ADAPTER_COUNT).astype(jnp.int32),
        "cached_lengths": draw_cached_lengths(jax.random.fold_in(jax.random.fold_in(key_list[12], part), 71), part),
        "request_page_tables": draw_request_page_tables(jax.random.fold_in(jax.random.fold_in(key_list[12], part), 71), part),
    }


theta_base = 500000.0
neg_large = -1e+30

def apply_rotation(values, token_positions, first_col, rot_limit):
    width_cols = values.shape[1]
    columns = first_col + jnp.arange(width_cols, dtype=jnp.int32)
    pair_index = (columns % HEAD_WIDTH // 2).astype(jnp.float32)
    inverse = jnp.exp(pair_index * (-2.0 * math.log(theta_base) / HEAD_WIDTH))
    angles = token_positions[:, None] * inverse[None, :]
    cos_val = jnp.cos(angles[:, 0::2])
    sine_val = jnp.sin(angles[:, 0::2])
    even_part = values[:, 0::2]
    odd_part = values[:, 1::2]
    turned = jnp.stack([even_part * cos_val - odd_part * sine_val, even_part * sine_val + odd_part * cos_val], axis=-1).reshape(values.shape)
    return jnp.where((columns < rot_limit)[None, :], turned, values)

def normalize(layer_input_tokens, input_norm_gain):
    values = layer_input_tokens.astype(jnp.float32)
    mean_square = lax.optimization_barrier(jnp.mean(values * values, axis=-1, keepdims=True))
    return (values * lax.rsqrt(mean_square + 1e-05) * input_norm_gain[None, :]).astype(jnp.bfloat16)

def positions_of(cached_lengths):
    steps_row = jnp.arange(NEW_TOKENS, dtype=jnp.int32)
    return (jnp.repeat(cached_lengths, NEW_TOKENS) + jnp.tile(steps_row, cached_lengths.shape[0])).astype(jnp.float32)

def reference(layer_input_tokens, input_norm_gain, query_weight, key_value_weight, output_weight, adapter_down_weight, adapter_up_weight, key_value_page_pool, request_adapter, adapter_storage_slot, cached_lengths, request_page_tables):
    normalized_input = normalize(layer_input_tokens, input_norm_gain)
    token_cache_slot = jnp.repeat(adapter_storage_slot[request_adapter], NEW_TOKENS).astype(jnp.int32)

    def down_one(inputs):
        token_input_row, storage_slot_index = inputs
        return jnp.dot(token_input_row[None, :], adapter_down_weight[storage_slot_index].T, preferred_element_type=jnp.float32)[0]
    adapter_choice_index = lax.map(down_one, (normalized_input, token_cache_slot)).astype(jnp.bfloat16)

    def single_up_weight(inputs):
        adapter_index_row, storage_slot_index = inputs
        return jnp.dot(adapter_index_row[None, :], adapter_up_weight[storage_slot_index], preferred_element_type=jnp.float32)[0]
    adapter_query_update = lax.map(single_up_weight, (adapter_choice_index, token_cache_slot))
    token_positions = positions_of(cached_lengths)
    query_vectors = apply_rotation(jnp.dot(normalized_input, query_weight, preferred_element_type=jnp.float32) + adapter_query_update, token_positions, 0, QUERY_WIDTH).astype(jnp.bfloat16)
    key_value_rows = apply_rotation(jnp.dot(normalized_input, key_value_weight, preferred_element_type=jnp.float32), token_positions, 0, KEY_VALUE_HEADS * HEAD_WIDTH).astype(jnp.bfloat16)
    query_group_width = QUERY_HEADS // KEY_VALUE_HEADS
    score_scale = 1.0 / math.sqrt(HEAD_WIDTH)
    causal = jnp.arange(NEW_TOKENS)[None, :] <= jnp.arange(NEW_TOKENS)[:, None]
    cache_position_span = MAXP * PAGE_LENGTH

    def attend(inputs):
        query_token_rows, incoming_rows, length, page_table_row = inputs
        page_contents = key_value_page_pool[jnp.maximum(page_table_row, 0)].reshape(cache_position_span, 2, KEY_VALUE_HEADS, HEAD_WIDTH).astype(jnp.float32)
        fresh_token_rows = incoming_rows.reshape(NEW_TOKENS, 2, KEY_VALUE_HEADS, HEAD_WIDTH).astype(jnp.float32)
        all_keys = jnp.concatenate([page_contents[:, 0], fresh_token_rows[:, 0]], axis=0)
        all_values = jnp.concatenate([page_contents[:, 1], fresh_token_rows[:, 1]], axis=0)
        query_head_split = query_token_rows.reshape(NEW_TOKENS, KEY_VALUE_HEADS, query_group_width, HEAD_WIDTH).astype(jnp.float32)
        scores = jnp.einsum('ikgd,lkd->ikgl', query_head_split, all_keys, precision=lax.Precision.HIGHEST) * score_scale
        cache_ok = jnp.arange(cache_position_span) < length
        key_valid = jnp.concatenate([jnp.broadcast_to(cache_ok[None, :], (NEW_TOKENS, cache_position_span)), causal], axis=1)
        valid_full = key_valid[:, None, None, :]
        masked = jnp.where(valid_full, scores, neg_large)
        row_peak = lax.optimization_barrier(jnp.max(masked, axis=-1, keepdims=True))
        weights = jnp.where(valid_full, jnp.exp(masked - row_peak), 0.0)
        row_total = lax.optimization_barrier(jnp.sum(weights, axis=-1))
        rounded = lax.optimization_barrier(weights.astype(jnp.bfloat16))
        mixture = jnp.einsum('ikgl,lkd->ikgd', rounded.astype(jnp.float32), all_values, precision=lax.Precision.HIGHEST)
        return (mixture / row_total[..., None]).reshape(NEW_TOKENS, QUERY_WIDTH).astype(jnp.bfloat16)
    attended = lax.map(attend, (query_vectors.reshape(REQS, NEW_TOKENS, QUERY_WIDTH), key_value_rows.reshape(REQS, NEW_TOKENS, KVW), cached_lengths, request_page_tables)).reshape(TOKENS, QUERY_WIDTH)
    return jnp.dot(attended, output_weight, preferred_element_type=jnp.float32).astype(jnp.bfloat16)
```

```python
import math

import jax
import jax.numpy as jnp
from jax import lax
from jax.sharding import PartitionSpec as P

QUERY_HEADS = 64
KEY_VALUE_HEADS = 8
HEAD_WIDTH = 128
PAGE_LENGTH = 128
NEW_TOKENS = 3


theta_base = 500000.0
neg_large = -1e30


def apply_rotation(values, token_positions, first_col, rot_limit):
    width_cols = values.shape[1]
    columns = first_col + jnp.arange(width_cols, dtype=jnp.int32)
    pair_index = (columns % HEAD_WIDTH // 2).astype(jnp.float32)
    inverse = jnp.exp(pair_index * (-2.0 * math.log(theta_base) / HEAD_WIDTH))
    angles = token_positions[:, None] * inverse[None, :]
    cos_val = jnp.cos(angles[:, 0::2])
    sine_val = jnp.sin(angles[:, 0::2])
    even_part = values[:, 0::2]
    odd_part = values[:, 1::2]
    turned = jnp.stack(
        [even_part * cos_val - odd_part * sine_val, even_part * sine_val + odd_part * cos_val],
        axis=-1,
    ).reshape(values.shape)
    return jnp.where((columns < rot_limit)[None, :], turned, values)


def normalize(layer_input_tokens, input_norm_gain):
    values = layer_input_tokens.astype(jnp.float32)
    mean_square = jnp.mean(values * values, axis=-1, keepdims=True)
    return (values * lax.rsqrt(mean_square + 1e-05) * input_norm_gain[None, :]).astype(jnp.bfloat16)


def positions_of(cached_lengths):
    steps_row = jnp.arange(NEW_TOKENS, dtype=jnp.int32)
    return (
        jnp.repeat(cached_lengths, NEW_TOKENS) + jnp.tile(steps_row, cached_lengths.shape[0])
    ).astype(jnp.float32)


def to_tokens(request_first_layout):
    request_count = request_first_layout.shape[0]
    trailing_shape = request_first_layout.shape[3:]
    query_group_width = QUERY_HEADS // KEY_VALUE_HEADS
    split_head_shape = request_first_layout.reshape(
        (request_count, KEY_VALUE_HEADS, NEW_TOKENS, query_group_width) + trailing_shape
    )
    order_axes = (0, 2, 1, 3) + tuple(range(4, 4 + len(trailing_shape)))
    return split_head_shape.transpose(order_axes).reshape(request_count * NEW_TOKENS, -1)


def butterfly(value, combine):
    size = lax.axis_size("blk")
    step = 1
    while step < size:
        pairs = [(i, i ^ step) for i in range(size)]
        value = combine(value, lax.ppermute(value, "blk", pairs))
        step *= 2
    return value


def local(
    layer_input_tokens,
    input_norm_gain,
    query_weight,
    key_value_weight,
    output_weight,
    adapter_down_weight,
    adapter_up_weight,
    key_value_page_pool,
    request_adapter,
    adapter_storage_slot,
    cached_lengths,
    request_page_tables,
):
    own_index = lax.axis_index("blk")
    gathered = lax.all_gather(layer_input_tokens, "blk", axis=1, tiled=True)
    normalized_input = normalize(gathered, input_norm_gain)
    request_count = cached_lengths.shape[0]
    adapter_total = adapter_storage_slot.shape[0]
    choose = request_adapter[:, None] == jnp.arange(adapter_total, dtype=jnp.int32)[None, :]
    req_slot = jnp.sum(jnp.where(choose, adapter_storage_slot[None, :], 0), axis=1)
    token_cache_slot = jnp.repeat(req_slot, NEW_TOKENS)
    local_token_count = adapter_down_weight.shape[0]
    local_pick = (
        token_cache_slot[:, None] - own_index * local_token_count
        == jnp.arange(local_token_count, dtype=jnp.int32)[None, :]
    )
    output_projected = jnp.einsum(
        "ly,mxy->lmx", normalized_input, adapter_down_weight, preferred_element_type=jnp.float32
    )
    partial_codes = jnp.sum(jnp.where(local_pick[:, :, None], output_projected, 0.0), axis=1)
    adapter_choice_index = butterfly(partial_codes.astype(jnp.bfloat16), jnp.add)
    up_weight_rows = adapter_up_weight[token_cache_slot]
    adapter_query_update = jnp.einsum(
        "gk,gkq->gq", adapter_choice_index, up_weight_rows, preferred_element_type=jnp.float32
    )
    token_positions = positions_of(cached_lengths)
    query_cols = query_weight.shape[1]
    keyval_cols = key_value_weight.shape[1]
    query_part = apply_rotation(
        jnp.dot(normalized_input, query_weight, preferred_element_type=jnp.float32)
        + adapter_query_update,
        token_positions,
        own_index * query_cols,
        QUERY_HEADS * HEAD_WIDTH,
    ).astype(jnp.bfloat16)
    keyval_part = apply_rotation(
        jnp.dot(normalized_input, key_value_weight, preferred_element_type=jnp.float32),
        token_positions,
        own_index * keyval_cols,
        KEY_VALUE_HEADS * HEAD_WIDTH,
    ).astype(jnp.bfloat16)
    joined = lax.all_gather(
        jnp.concatenate([query_part, keyval_part], axis=1), "blk", axis=1, tiled=False
    )
    query_vectors = joined[:, :, :query_cols].reshape(joined.shape[0], -1)
    key_value_rows = joined[:, :, query_cols:].reshape(joined.shape[0], -1)
    query_group_width = QUERY_HEADS // KEY_VALUE_HEADS
    query_feature_width = query_group_width * NEW_TOKENS
    score_scale = 1.0 / math.sqrt(HEAD_WIDTH)
    query_req = (
        query_vectors.reshape(
            request_count, NEW_TOKENS, KEY_VALUE_HEADS, query_group_width, HEAD_WIDTH
        )
        .transpose(0, 2, 1, 3, 4)
        .reshape(request_count, KEY_VALUE_HEADS, query_feature_width, HEAD_WIDTH)
    )
    fresh_token_rows = key_value_rows.reshape(
        request_count, NEW_TOKENS, 2, KEY_VALUE_HEADS, HEAD_WIDTH
    )
    request_page_count = key_value_page_pool.shape[0]
    table_width = request_page_tables.shape[1]
    page_ids = own_index * request_page_count + jnp.arange(request_page_count, dtype=jnp.int32)
    matches = request_page_tables[None, :, :] == page_ids[:, None, None]
    page_owner = jnp.any(matches, axis=2)
    page_live = jnp.any(page_owner, axis=1)
    page_req = jnp.sum(
        jnp.where(page_owner, jnp.arange(request_count, dtype=jnp.int32)[None, :], 0), axis=1
    )
    page_slot = jnp.sum(
        jnp.where(matches, jnp.arange(table_width, dtype=jnp.int32)[None, None, :], 0), axis=(1, 2)
    )
    page_len = jnp.sum(jnp.where(page_owner, cached_lengths[None, :], 0), axis=1)
    key_pos = page_slot[:, None] * PAGE_LENGTH + jnp.arange(PAGE_LENGTH, dtype=jnp.int32)[None, :]
    key_valid = page_live[:, None] & (key_pos < page_len[:, None])
    valid_full = key_valid[:, None, None, :]
    gathered_cache_pages = key_value_page_pool.reshape(
        request_page_count, PAGE_LENGTH, 2, KEY_VALUE_HEADS, HEAD_WIDTH
    )
    query_page = query_req[page_req]
    scores = (
        jnp.einsum(
            "skqd,spkd->skqp",
            query_page,
            gathered_cache_pages[:, :, 0],
            preferred_element_type=jnp.float32,
        )
        * score_scale
    )
    masked = jnp.where(valid_full, scores, neg_large)
    page_peak = jnp.max(masked, axis=-1)
    req_peak = jnp.max(
        jnp.where(page_owner[:, :, None, None], page_peak[:, None], neg_large), axis=0
    )
    fresh_scores = (
        jnp.einsum(
            "rkqd,rjkd->rkqj",
            query_req,
            fresh_token_rows[:, :, 0],
            preferred_element_type=jnp.float32,
        )
        * score_scale
    )
    step_of = jnp.arange(query_feature_width, dtype=jnp.int32) // query_group_width
    fresh_ok = (jnp.arange(NEW_TOKENS, dtype=jnp.int32)[None, :] <= step_of[:, None])[None, None]
    fresh_masked = jnp.where(fresh_ok, fresh_scores, neg_large)
    top_score = butterfly(jnp.maximum(req_peak, jnp.max(fresh_masked, axis=-1)), jnp.maximum)
    weights = jnp.where(valid_full, jnp.exp(masked - top_score[page_req][..., None]), 0.0)
    page_num = jnp.einsum(
        "skqp,spkd->skqd",
        weights.astype(jnp.bfloat16),
        gathered_cache_pages[:, :, 1],
        preferred_element_type=jnp.float32,
    )
    owner_frac = page_owner.astype(jnp.float32)
    req_num = jnp.einsum("sr,skqd->rkqd", owner_frac, page_num, precision=lax.Precision.HIGHEST)
    req_den = jnp.einsum(
        "sr,skq->rkq", owner_frac, jnp.sum(weights, axis=-1), precision=lax.Precision.HIGHEST
    )
    fresh_weights = jnp.where(fresh_ok, jnp.exp(fresh_masked - top_score[..., None]), 0.0)
    fresh_num = jnp.einsum(
        "rkqj,rjkd->rkqd",
        fresh_weights.astype(jnp.bfloat16),
        fresh_token_rows[:, :, 1],
        preferred_element_type=jnp.float32,
    )
    fresh_den = jnp.sum(fresh_weights, axis=-1)
    num_tok = to_tokens(req_num)
    den_tok = to_tokens(req_den[..., None])
    fresh_num_tok = to_tokens(fresh_num)
    fresh_den_tok = to_tokens(fresh_den[..., None])
    pad_width = HEAD_WIDTH - den_tok.shape[1] % HEAD_WIDTH
    summed = lax.psum(
        jnp.concatenate([num_tok, den_tok, jnp.zeros((den_tok.shape[0], pad_width), jnp.float32)], axis=1),
        "blk",
    )
    num_all = summed[:, : num_tok.shape[1]]
    den_all = summed[:, num_tok.shape[1] : num_tok.shape[1] + den_tok.shape[1]]
    totals = den_all + fresh_den_tok
    attended = ((num_all + fresh_num_tok) / jnp.repeat(totals, HEAD_WIDTH, axis=1)).astype(
        jnp.bfloat16
    )
    return jnp.dot(attended, output_weight, preferred_element_type=jnp.float32).astype(jnp.bfloat16)


def solution(mesh):
    placed = (
        P("groups", "blk"),
        P(),
        P(None, "blk"),
        P(None, "blk"),
        P(None, "blk"),
        P("blk", None, None),
        P(None, None, "blk"),
        P(("groups", "blk"), None, None),
        P("groups"),
        P(),
        P("groups"),
        P("groups", None),
    )
    return jax.shard_map(
        local, mesh=mesh, in_specs=placed, out_specs=P("groups", "blk"), check_vma=False
    )
```

```python
import math

import jax
import jax.numpy as jnp
from jax import lax
from jax.sharding import PartitionSpec as P

QUERY_HEADS = 64
KEY_VALUE_HEADS = 8
HEAD_WIDTH = 128
PAGE_LENGTH = 128
NEW_TOKENS = 3


theta_base = 500000.0
neg_large = -1e30


def apply_rotation(values, token_positions, first_col, rot_limit):
    width_cols = values.shape[1]
    columns = first_col + jnp.arange(width_cols, dtype=jnp.int32)
    pair_index = (columns % HEAD_WIDTH // 2).astype(jnp.float32)
    inverse = jnp.exp(pair_index * (-2.0 * math.log(theta_base) / HEAD_WIDTH))
    angles = token_positions[:, None] * inverse[None, :]
    cos_val = jnp.cos(angles[:, 0::2])
    sine_val = jnp.sin(angles[:, 0::2])
    even_part = values[:, 0::2]
    odd_part = values[:, 1::2]
    turned = jnp.stack(
        [even_part * cos_val - odd_part * sine_val, even_part * sine_val + odd_part * cos_val],
        axis=-1,
    ).reshape(values.shape)
    return jnp.where((columns < rot_limit)[None, :], turned, values)


def normalize(layer_input_tokens, input_norm_gain):
    values = layer_input_tokens.astype(jnp.float32)
    mean_square = jnp.mean(values * values, axis=-1, keepdims=True)
    return (values * lax.rsqrt(mean_square + 1e-05) * input_norm_gain[None, :]).astype(jnp.bfloat16)


def positions_of(cached_lengths):
    steps_row = jnp.arange(NEW_TOKENS, dtype=jnp.int32)
    return (
        jnp.repeat(cached_lengths, NEW_TOKENS) + jnp.tile(steps_row, cached_lengths.shape[0])
    ).astype(jnp.float32)


def to_tokens(request_first_layout):
    request_count = request_first_layout.shape[0]
    trailing_shape = request_first_layout.shape[3:]
    query_group_width = QUERY_HEADS // KEY_VALUE_HEADS
    split_head_shape = request_first_layout.reshape(
        (request_count, KEY_VALUE_HEADS, NEW_TOKENS, query_group_width) + trailing_shape
    )
    order_axes = (0, 2, 1, 3) + tuple(range(4, 4 + len(trailing_shape)))
    return split_head_shape.transpose(order_axes).reshape(request_count * NEW_TOKENS, -1)


def butterfly(value, combine):
    size = lax.axis_size("blk")
    step = 1
    while step < size:
        pairs = [(i, i ^ step) for i in range(size)]
        value = combine(value, lax.ppermute(value, "blk", pairs))
        step *= 2
    return value


def local(
    layer_input_tokens,
    input_norm_gain,
    query_weight,
    key_value_weight,
    output_weight,
    adapter_down_weight,
    adapter_up_weight,
    key_value_page_pool,
    request_adapter,
    adapter_storage_slot,
    cached_lengths,
    request_page_tables,
):
    own_index = lax.axis_index("blk")
    gathered = lax.all_gather(layer_input_tokens, "blk", axis=1, tiled=True)
    normalized_input = normalize(gathered, input_norm_gain)
    request_count = cached_lengths.shape[0]
    adapter_total = adapter_storage_slot.shape[0]
    choose = request_adapter[:, None] == jnp.arange(adapter_total, dtype=jnp.int32)[None, :]
    req_slot = jnp.sum(jnp.where(choose, adapter_storage_slot[None, :], 0), axis=1)
    token_cache_slot = jnp.repeat(req_slot, NEW_TOKENS)
    local_token_count = adapter_down_weight.shape[0]
    local_pick = (
        token_cache_slot[:, None] - own_index * local_token_count
        == jnp.arange(local_token_count, dtype=jnp.int32)[None, :]
    )
    output_projected = jnp.einsum(
        "ly,mxy->lmx", normalized_input, adapter_down_weight, preferred_element_type=jnp.float32
    )
    partial_codes = jnp.sum(jnp.where(local_pick[:, :, None], output_projected, 0.0), axis=1)
    adapter_choice_index = butterfly(partial_codes.astype(jnp.bfloat16), jnp.add)
    up_weight_rows = adapter_up_weight[token_cache_slot]
    adapter_query_update = jnp.einsum(
        "gk,gkq->gq", adapter_choice_index, up_weight_rows, preferred_element_type=jnp.float32
    )
    token_positions = positions_of(cached_lengths)
    query_cols = query_weight.shape[1]
    keyval_cols = key_value_weight.shape[1]
    query_part = apply_rotation(
        jnp.dot(normalized_input, query_weight, preferred_element_type=jnp.float32)
        + adapter_query_update,
        token_positions,
        own_index * query_cols,
        QUERY_HEADS * HEAD_WIDTH,
    ).astype(jnp.bfloat16)
    keyval_part = apply_rotation(
        jnp.dot(normalized_input, key_value_weight, preferred_element_type=jnp.float32),
        token_positions,
        own_index * keyval_cols,
        KEY_VALUE_HEADS * HEAD_WIDTH,
    ).astype(jnp.bfloat16)
    joined = lax.all_gather(
        jnp.concatenate([query_part, keyval_part], axis=1), "blk", axis=1, tiled=False
    )
    query_vectors = joined[:, :, :query_cols].reshape(joined.shape[0], -1)
    key_value_rows = joined[:, :, query_cols:].reshape(joined.shape[0], -1)
    query_group_width = QUERY_HEADS // KEY_VALUE_HEADS
    query_feature_width = query_group_width * NEW_TOKENS
    score_scale = 1.0 / math.sqrt(HEAD_WIDTH)
    query_req = (
        query_vectors.reshape(
            request_count, NEW_TOKENS, KEY_VALUE_HEADS, query_group_width, HEAD_WIDTH
        )
        .transpose(0, 2, 1, 3, 4)
        .reshape(request_count, KEY_VALUE_HEADS, query_feature_width, HEAD_WIDTH)
    )
    fresh_token_rows = key_value_rows.reshape(
        request_count, NEW_TOKENS, 2, KEY_VALUE_HEADS, HEAD_WIDTH
    )
    request_page_count = key_value_page_pool.shape[0]
    table_width = request_page_tables.shape[1]
    page_ids = own_index * request_page_count + jnp.arange(request_page_count, dtype=jnp.int32)
    matches = request_page_tables[None, :, :] == page_ids[:, None, None]
    page_owner = jnp.any(matches, axis=2)
    page_live = jnp.any(page_owner, axis=1)
    page_req = jnp.sum(
        jnp.where(page_owner, jnp.arange(request_count, dtype=jnp.int32)[None, :], 0), axis=1
    )
    page_slot = jnp.sum(
        jnp.where(matches, jnp.arange(table_width, dtype=jnp.int32)[None, None, :], 0), axis=(1, 2)
    )
    page_len = jnp.sum(jnp.where(page_owner, cached_lengths[None, :], 0), axis=1)
    key_pos = page_slot[:, None] * PAGE_LENGTH + jnp.arange(PAGE_LENGTH, dtype=jnp.int32)[None, :]
    key_valid = page_live[:, None] & (key_pos < page_len[:, None])
    valid_full = key_valid[:, None, None, :]
    gathered_cache_pages = key_value_page_pool.reshape(
        request_page_count, PAGE_LENGTH, 2, KEY_VALUE_HEADS, HEAD_WIDTH
    )
    query_page = query_req[page_req]
    scores = (
        jnp.einsum(
            "skqd,spkd->skqp",
            query_page,
            gathered_cache_pages[:, :, 0],
            preferred_element_type=jnp.float32,
        )
        * score_scale
    )
    masked = jnp.where(valid_full, scores, neg_large)
    page_peak = jnp.max(masked, axis=-1)
    req_peak = jnp.max(
        jnp.where(page_owner[:, :, None, None], page_peak[:, None], neg_large), axis=0
    )
    fresh_scores = (
        jnp.einsum(
            "rkqd,rjkd->rkqj",
            query_req,
            fresh_token_rows[:, :, 0],
            preferred_element_type=jnp.float32,
        )
        * score_scale
    )
    step_of = jnp.arange(query_feature_width, dtype=jnp.int32) // query_group_width
    fresh_ok = (jnp.arange(NEW_TOKENS, dtype=jnp.int32)[None, :] <= step_of[:, None])[None, None]
    fresh_masked = jnp.where(fresh_ok, fresh_scores, neg_large)
    top_score = butterfly(jnp.maximum(req_peak, jnp.max(fresh_masked, axis=-1)), jnp.maximum)
    weights = jnp.where(valid_full, jnp.exp(masked - top_score[page_req][..., None]), 0.0)
    page_num = jnp.einsum(
        "skqp,spkd->skqd",
        weights.astype(jnp.bfloat16),
        gathered_cache_pages[:, :, 1],
        preferred_element_type=jnp.float32,
    )
    device_count = lax.axis_size("blk")
    head_count = QUERY_HEADS
    owner_cols = query_cols
    owner_heads = max(1, owner_cols // HEAD_WIDTH)
    head_repeat = min(owner_cols, HEAD_WIDTH)
    owner_first_head = [(o * owner_cols) // HEAD_WIDTH for o in range(device_count)]
    head_pick = jnp.asarray(
        [[first + j for j in range(owner_heads)] for first in owner_first_head], jnp.int32
    )
    slot_num = to_tokens(page_num).reshape(request_page_count, NEW_TOKENS, device_count, owner_cols)
    slot_den = to_tokens(jnp.sum(weights, axis=-1)[..., None]).reshape(
        request_page_count, NEW_TOKENS, head_count
    )
    slot_den_owner = slot_den[:, :, head_pick]
    packed = jnp.concatenate([slot_num, slot_den_owner], axis=3).transpose(2, 0, 1, 3)
    received = lax.all_to_all(packed, "blk", 0, 0, tiled=True)
    group_pages = device_count * request_page_count
    all_page_ids = jnp.arange(group_pages, dtype=jnp.int32)
    all_owner = jnp.any(request_page_tables[None, :, :] == all_page_ids[:, None, None], axis=2)
    pick_req = all_owner.T.astype(jnp.float32)
    summed = jnp.einsum(
        "rp,px->rx",
        pick_req,
        received.reshape(group_pages, -1),
        precision=lax.Precision.HIGHEST,
    ).reshape(request_count, NEW_TOKENS, owner_cols + owner_heads)
    fresh_weights = jnp.where(fresh_ok, jnp.exp(fresh_masked - top_score[..., None]), 0.0)
    fresh_num = jnp.einsum(
        "rkqj,rjkd->rkqd",
        fresh_weights.astype(jnp.bfloat16),
        fresh_token_rows[:, :, 1],
        preferred_element_type=jnp.float32,
    )
    fresh_den = jnp.sum(fresh_weights, axis=-1)
    fresh_num_own = lax.dynamic_slice_in_dim(
        to_tokens(fresh_num), own_index * owner_cols, owner_cols, axis=1
    )
    fresh_den_own = lax.dynamic_slice_in_dim(
        to_tokens(fresh_den[..., None]), (own_index * owner_cols) // HEAD_WIDTH, owner_heads, axis=1
    )
    num_own = summed[:, :, :owner_cols].reshape(request_count * NEW_TOKENS, owner_cols)
    den_own = summed[:, :, owner_cols:].reshape(request_count * NEW_TOKENS, owner_heads)
    totals = den_own + fresh_den_own
    attended_own = ((num_own + fresh_num_own) / jnp.repeat(totals, head_repeat, axis=1)).astype(
        jnp.bfloat16
    )
    attended = lax.all_gather(attended_own, "blk", axis=1, tiled=True)
    return jnp.dot(attended, output_weight, preferred_element_type=jnp.float32).astype(jnp.bfloat16)


def solution(mesh):
    placed = (
        P("groups", "blk"),
        P(),
        P(None, "blk"),
        P(None, "blk"),
        P(None, "blk"),
        P("blk", None, None),
        P(None, None, "blk"),
        P(("groups", "blk"), None, None),
        P("groups"),
        P(),
        P("groups"),
        P("groups", None),
    )
    return jax.shard_map(
        local, mesh=mesh, in_specs=placed, out_specs=P("groups", "blk"), check_vma=False
    )
```

```python
import math

import jax
import jax.numpy as jnp
from jax import lax
from jax.experimental import pallas as pl
from jax.experimental.pallas import tpu as pltpu
from jax.sharding import PartitionSpec as P

QUERY_HEADS = 64
KEY_VALUE_HEADS = 8
HEAD_WIDTH = 128
PAGE_LENGTH = 128
NEW_TOKENS = 3


theta_base = 500000.0
neg_large = -1e30


def apply_rotation(values, token_positions, first_col, rot_limit):
    width_cols = values.shape[1]
    columns = first_col + jnp.arange(width_cols, dtype=jnp.int32)
    pair_index = (columns % HEAD_WIDTH // 2).astype(jnp.float32)
    inverse = jnp.exp(pair_index * (-2.0 * math.log(theta_base) / HEAD_WIDTH))
    angles = token_positions[:, None] * inverse[None, :]
    cos_val = jnp.cos(angles[:, 0::2])
    sine_val = jnp.sin(angles[:, 0::2])
    even_part = values[:, 0::2]
    odd_part = values[:, 1::2]
    turned = jnp.stack(
        [even_part * cos_val - odd_part * sine_val, even_part * sine_val + odd_part * cos_val],
        axis=-1,
    ).reshape(values.shape)
    return jnp.where((columns < rot_limit)[None, :], turned, values)


def rotation_kernel(values_ref, cos_ref, sine_ref, out_ref):
    values = values_ref[...]
    width = values.shape[1]
    following = pltpu.roll(values, width - 1, 1)
    preceding = pltpu.roll(values, 1, 1)
    even = lax.broadcasted_iota(jnp.int32, values.shape, 1) % 2 == 0
    cos_val = cos_ref[...]
    sine_val = sine_ref[...]
    out_ref[...] = jnp.where(
        even, values * cos_val - following * sine_val, preceding * sine_val + values * cos_val
    ).astype(out_ref.dtype)


def rotate_columns(values, token_positions, global_cols, rot_limit):
    pair_index = (global_cols % HEAD_WIDTH // 2).astype(jnp.float32)
    inverse = jnp.exp(pair_index * (-2.0 * math.log(theta_base) / HEAD_WIDTH))
    angles = token_positions[:, None] * inverse[None, :]
    rotated = (global_cols < rot_limit)[None, :]
    cos_val = jnp.where(rotated, jnp.cos(angles), 1.0)
    sine_val = jnp.where(rotated, jnp.sin(angles), 0.0)
    width = values.shape[1]
    pad = -(-width // 128) * 128 - width
    operands = [jnp.pad(a, ((0, 0), (0, pad))) for a in (values, cos_val, sine_val)]
    out = pl.pallas_call(
        rotation_kernel,
        out_shape=jax.ShapeDtypeStruct(operands[0].shape, jnp.bfloat16),
    )(*operands)
    return out[:, :width]


def normalize(layer_input_tokens, input_norm_gain):
    values = layer_input_tokens.astype(jnp.float32)
    mean_square = jnp.mean(values * values, axis=-1, keepdims=True)
    return (values * lax.rsqrt(mean_square + 1e-05) * input_norm_gain[None, :]).astype(jnp.bfloat16)


def positions_of(cached_lengths):
    steps_row = jnp.arange(NEW_TOKENS, dtype=jnp.int32)
    return (
        jnp.repeat(cached_lengths, NEW_TOKENS) + jnp.tile(steps_row, cached_lengths.shape[0])
    ).astype(jnp.float32)


def to_tokens(request_first_layout):
    request_count = request_first_layout.shape[0]
    trailing_shape = request_first_layout.shape[3:]
    query_group_width = QUERY_HEADS // KEY_VALUE_HEADS
    split_head_shape = request_first_layout.reshape(
        (request_count, KEY_VALUE_HEADS, NEW_TOKENS, query_group_width) + trailing_shape
    )
    order_axes = (0, 2, 1, 3) + tuple(range(4, 4 + len(trailing_shape)))
    return split_head_shape.transpose(order_axes).reshape(request_count * NEW_TOKENS, -1)


def butterfly(value, combine):
    size = lax.axis_size("blk")
    step = 1
    while step < size:
        pairs = [(i, i ^ step) for i in range(size)]
        value = combine(value, lax.ppermute(value, "blk", pairs))
        step *= 2
    return value


def local(
    layer_input_tokens,
    input_norm_gain,
    query_weight,
    key_value_weight,
    output_weight,
    adapter_down_weight,
    adapter_up_weight,
    key_value_page_pool,
    request_adapter,
    adapter_storage_slot,
    cached_lengths,
    request_page_tables,
):
    own_index = lax.axis_index("blk")
    gathered = lax.all_gather(layer_input_tokens, "blk", axis=1, tiled=True)
    normalized_input = normalize(gathered, input_norm_gain)
    request_count = cached_lengths.shape[0]
    adapter_total = adapter_storage_slot.shape[0]
    choose = request_adapter[:, None] == jnp.arange(adapter_total, dtype=jnp.int32)[None, :]
    req_slot = jnp.sum(jnp.where(choose, adapter_storage_slot[None, :], 0), axis=1)
    token_cache_slot = jnp.repeat(req_slot, NEW_TOKENS)
    local_token_count = adapter_down_weight.shape[0]
    local_pick = (
        token_cache_slot[:, None] - own_index * local_token_count
        == jnp.arange(local_token_count, dtype=jnp.int32)[None, :]
    )
    output_projected = jnp.einsum(
        "ly,mxy->lmx", normalized_input, adapter_down_weight, preferred_element_type=jnp.float32
    )
    partial_codes = jnp.sum(jnp.where(local_pick[:, :, None], output_projected, 0.0), axis=1)
    adapter_choice_index = butterfly(partial_codes.astype(jnp.bfloat16), jnp.add)
    up_weight_rows = adapter_up_weight[token_cache_slot]
    adapter_query_update = jnp.einsum(
        "gk,gkq->gq", adapter_choice_index, up_weight_rows, preferred_element_type=jnp.float32
    )
    token_positions = positions_of(cached_lengths)
    query_cols = query_weight.shape[1]
    keyval_cols = key_value_weight.shape[1]
    both_parts = jnp.concatenate(
        [
            jnp.dot(normalized_input, query_weight, preferred_element_type=jnp.float32)
            + adapter_query_update,
            jnp.dot(normalized_input, key_value_weight, preferred_element_type=jnp.float32),
        ],
        axis=1,
    )
    global_cols = jnp.concatenate(
        [
            own_index * query_cols + jnp.arange(query_cols, dtype=jnp.int32),
            own_index * keyval_cols + jnp.arange(keyval_cols, dtype=jnp.int32),
        ]
    )
    limits = jnp.concatenate(
        [
            jnp.full((query_cols,), QUERY_HEADS * HEAD_WIDTH, jnp.int32),
            jnp.full((keyval_cols,), KEY_VALUE_HEADS * HEAD_WIDTH, jnp.int32),
        ]
    )
    rotated_parts = rotate_columns(both_parts, token_positions, global_cols, limits)
    joined = lax.all_gather(rotated_parts, "blk", axis=1, tiled=False)
    query_vectors = joined[:, :, :query_cols].reshape(joined.shape[0], -1)
    key_value_rows = joined[:, :, query_cols:].reshape(joined.shape[0], -1)
    query_group_width = QUERY_HEADS // KEY_VALUE_HEADS
    query_feature_width = query_group_width * NEW_TOKENS
    score_scale = 1.0 / math.sqrt(HEAD_WIDTH)
    query_split = query_vectors.reshape(
        request_count, NEW_TOKENS, KEY_VALUE_HEADS, query_group_width, HEAD_WIDTH
    )
    fresh_token_rows = key_value_rows.reshape(
        request_count, NEW_TOKENS, 2, KEY_VALUE_HEADS, HEAD_WIDTH
    )
    request_page_count = key_value_page_pool.shape[0]
    table_width = request_page_tables.shape[1]
    page_ids = own_index * request_page_count + jnp.arange(request_page_count, dtype=jnp.int32)
    matches = request_page_tables[None, :, :] == page_ids[:, None, None]
    page_owner = jnp.any(matches, axis=2)
    page_live = jnp.any(page_owner, axis=1)
    page_req = jnp.sum(
        jnp.where(page_owner, jnp.arange(request_count, dtype=jnp.int32)[None, :], 0), axis=1
    )
    page_slot = jnp.sum(
        jnp.where(matches, jnp.arange(table_width, dtype=jnp.int32)[None, None, :], 0), axis=(1, 2)
    )
    page_len = jnp.sum(jnp.where(page_owner, cached_lengths[None, :], 0), axis=1)
    key_pos = page_slot[:, None] * PAGE_LENGTH + jnp.arange(PAGE_LENGTH, dtype=jnp.int32)[None, :]
    key_valid = page_live[:, None] & (key_pos < page_len[:, None])
    valid_full = key_valid[:, None, None, :]
    gathered_cache_pages = key_value_page_pool.reshape(
        request_page_count, PAGE_LENGTH, 2, KEY_VALUE_HEADS, HEAD_WIDTH
    )
    query_page = (
        query_split[page_req]
        .transpose(0, 2, 1, 3, 4)
        .reshape(request_page_count, KEY_VALUE_HEADS, query_feature_width, HEAD_WIDTH)
    )
    scores = (
        jnp.einsum(
            "skqd,spkd->skqp",
            query_page,
            gathered_cache_pages[:, :, 0],
            preferred_element_type=jnp.float32,
        )
        * score_scale
    )
    masked = jnp.where(valid_full, scores, neg_large)
    page_peak = jnp.max(masked, axis=-1)
    req_peak = jnp.max(
        jnp.where(page_owner[:, :, None, None], page_peak[:, None], neg_large), axis=0
    )
    query_wide = query_split.astype(jnp.float32)
    fresh_keys = fresh_token_rows[:, :, 0].astype(jnp.float32)
    fresh_scores = (
        jnp.stack(
            [
                jnp.sum(query_wide * fresh_keys[:, j][:, None, :, None, :], axis=-1)
                for j in range(NEW_TOKENS)
            ],
            axis=-1,
        )
        .transpose(0, 2, 1, 3, 4)
        .reshape(request_count, KEY_VALUE_HEADS, query_feature_width, NEW_TOKENS)
        * score_scale
    )
    step_of = jnp.arange(query_feature_width, dtype=jnp.int32) // query_group_width
    fresh_ok = (jnp.arange(NEW_TOKENS, dtype=jnp.int32)[None, :] <= step_of[:, None])[None, None]
    fresh_masked = jnp.where(fresh_ok, fresh_scores, neg_large)
    top_score = butterfly(jnp.maximum(req_peak, jnp.max(fresh_masked, axis=-1)), jnp.maximum)
    weights = jnp.where(valid_full, jnp.exp(masked - top_score[page_req][..., None]), 0.0)
    page_num = jnp.einsum(
        "skqp,spkd->skqd",
        weights.astype(jnp.bfloat16),
        gathered_cache_pages[:, :, 1],
        preferred_element_type=jnp.float32,
    )
    device_count = lax.axis_size("blk")
    head_count = QUERY_HEADS
    owner_cols = query_cols
    owner_heads = max(1, owner_cols // HEAD_WIDTH)
    head_repeat = min(owner_cols, HEAD_WIDTH)
    owner_first_head = [(o * owner_cols) // HEAD_WIDTH for o in range(device_count)]
    head_pick = jnp.asarray(
        [[first + j for j in range(owner_heads)] for first in owner_first_head], jnp.int32
    )
    slot_num = to_tokens(page_num).reshape(request_page_count, NEW_TOKENS, device_count, owner_cols)
    slot_den = to_tokens(jnp.sum(weights, axis=-1)[..., None]).reshape(
        request_page_count, NEW_TOKENS, head_count
    )
    slot_den_owner = slot_den[:, :, head_pick]
    packed = jnp.concatenate([slot_num, slot_den_owner], axis=3).transpose(2, 0, 1, 3)
    received = lax.all_to_all(packed, "blk", 0, 0, tiled=True)
    group_pages = device_count * request_page_count
    all_page_ids = jnp.arange(group_pages, dtype=jnp.int32)
    all_owner = jnp.any(request_page_tables[None, :, :] == all_page_ids[:, None, None], axis=2)
    pick_req = all_owner.T.astype(jnp.float32)
    summed = jnp.einsum(
        "rp,px->rx",
        pick_req,
        received.reshape(group_pages, -1),
        precision=lax.Precision.HIGHEST,
    ).reshape(request_count, NEW_TOKENS, owner_cols + owner_heads)
    fresh_weights = jnp.where(fresh_ok, jnp.exp(fresh_masked - top_score[..., None]), 0.0)
    fresh_by_head = (
        fresh_weights.reshape(
            request_count, KEY_VALUE_HEADS, NEW_TOKENS, query_group_width, NEW_TOKENS
        )
        .transpose(0, 2, 1, 3, 4)
        .reshape(request_count, NEW_TOKENS, QUERY_HEADS, NEW_TOKENS)
    )
    first_head = (own_index * owner_cols) // HEAD_WIDTH
    weights_own = lax.dynamic_slice_in_dim(fresh_by_head, first_head, owner_heads, axis=2)
    value_col = (
        KEY_VALUE_HEADS * HEAD_WIDTH
        + (first_head // query_group_width) * HEAD_WIDTH
        + (own_index * owner_cols) % HEAD_WIDTH
    )
    values_own = lax.dynamic_slice_in_dim(
        key_value_rows.reshape(request_count, NEW_TOKENS, -1), value_col, head_repeat, axis=2
    )
    fresh_num_own = jnp.einsum(
        "rihj,rjd->rihd",
        weights_own.astype(jnp.bfloat16),
        values_own,
        preferred_element_type=jnp.float32,
    ).reshape(request_count * NEW_TOKENS, owner_cols)
    fresh_den_own = jnp.sum(weights_own, axis=-1).reshape(request_count * NEW_TOKENS, owner_heads)
    num_own = summed[:, :, :owner_cols].reshape(request_count * NEW_TOKENS, owner_cols)
    den_own = summed[:, :, owner_cols:].reshape(request_count * NEW_TOKENS, owner_heads)
    totals = den_own + fresh_den_own
    attended_own = ((num_own + fresh_num_own) / jnp.repeat(totals, head_repeat, axis=1)).astype(
        jnp.bfloat16
    )
    attended = lax.all_gather(attended_own, "blk", axis=1, tiled=True)
    return jnp.dot(attended, output_weight, preferred_element_type=jnp.float32).astype(jnp.bfloat16)


def solution(mesh):
    placed = (
        P("groups", "blk"),
        P(),
        P(None, "blk"),
        P(None, "blk"),
        P(None, "blk"),
        P("blk", None, None),
        P(None, None, "blk"),
        P(("groups", "blk"), None, None),
        P("groups"),
        P(),
        P("groups"),
        P("groups", None),
    )
    return jax.shard_map(
        local, mesh=mesh, in_specs=placed, out_specs=P("groups", "blk"), check_vma=False
    )
```

```python
import math

import jax
import jax.numpy as jnp
from jax import lax
from jax.experimental import pallas as pl
from jax.experimental.pallas import tpu as pltpu
from jax.sharding import PartitionSpec as P

QUERY_HEADS = 64
KEY_VALUE_HEADS = 8
HEAD_WIDTH = 128
PAGE_LENGTH = 128
NEW_TOKENS = 3


theta_base = 500000.0
neg_large = -1e30


def apply_rotation(values, token_positions, first_col, rot_limit):
    width_cols = values.shape[1]
    columns = first_col + jnp.arange(width_cols, dtype=jnp.int32)
    pair_index = (columns % HEAD_WIDTH // 2).astype(jnp.float32)
    inverse = jnp.exp(pair_index * (-2.0 * math.log(theta_base) / HEAD_WIDTH))
    angles = token_positions[:, None] * inverse[None, :]
    cos_val = jnp.cos(angles[:, 0::2])
    sine_val = jnp.sin(angles[:, 0::2])
    even_part = values[:, 0::2]
    odd_part = values[:, 1::2]
    turned = jnp.stack(
        [even_part * cos_val - odd_part * sine_val, even_part * sine_val + odd_part * cos_val],
        axis=-1,
    ).reshape(values.shape)
    return jnp.where((columns < rot_limit)[None, :], turned, values)


def rotation_kernel(values_ref, cos_ref, sine_ref, out_ref):
    values = values_ref[...]
    width = values.shape[1]
    following = pltpu.roll(values, width - 1, 1)
    preceding = pltpu.roll(values, 1, 1)
    even = lax.broadcasted_iota(jnp.int32, values.shape, 1) % 2 == 0
    cos_val = cos_ref[...]
    sine_val = sine_ref[...]
    out_ref[...] = jnp.where(
        even, values * cos_val - following * sine_val, preceding * sine_val + values * cos_val
    ).astype(out_ref.dtype)


def rotate_columns(values, token_positions, global_cols, rot_limit):
    pair_index = (global_cols % HEAD_WIDTH // 2).astype(jnp.float32)
    inverse = jnp.exp(pair_index * (-2.0 * math.log(theta_base) / HEAD_WIDTH))
    angles = token_positions[:, None] * inverse[None, :]
    rotated = (global_cols < rot_limit)[None, :]
    cos_val = jnp.where(rotated, jnp.cos(angles), 1.0)
    sine_val = jnp.where(rotated, jnp.sin(angles), 0.0)
    width = values.shape[1]
    pad = -(-width // 128) * 128 - width
    operands = [jnp.pad(a, ((0, 0), (0, pad))) for a in (values, cos_val, sine_val)]
    out = pl.pallas_call(
        rotation_kernel,
        out_shape=jax.ShapeDtypeStruct(operands[0].shape, jnp.bfloat16),
    )(*operands)
    return out[:, :width]


def normalize(layer_input_tokens, input_norm_gain):
    values = layer_input_tokens.astype(jnp.float32)
    mean_square = jnp.mean(values * values, axis=-1, keepdims=True)
    return (values * lax.rsqrt(mean_square + 1e-05) * input_norm_gain[None, :]).astype(jnp.bfloat16)


def positions_of(cached_lengths):
    steps_row = jnp.arange(NEW_TOKENS, dtype=jnp.int32)
    return (
        jnp.repeat(cached_lengths, NEW_TOKENS) + jnp.tile(steps_row, cached_lengths.shape[0])
    ).astype(jnp.float32)


def to_tokens(request_first_layout):
    request_count = request_first_layout.shape[0]
    trailing_shape = request_first_layout.shape[3:]
    query_group_width = QUERY_HEADS // KEY_VALUE_HEADS
    split_head_shape = request_first_layout.reshape(
        (request_count, KEY_VALUE_HEADS, NEW_TOKENS, query_group_width) + trailing_shape
    )
    order_axes = (0, 2, 1, 3) + tuple(range(4, 4 + len(trailing_shape)))
    return split_head_shape.transpose(order_axes).reshape(request_count * NEW_TOKENS, -1)


def butterfly(value, combine):
    size = lax.axis_size("blk")
    step = 1
    while step < size:
        masks = [step] if step * 2 >= size else [step, step * 2, step * 3]
        arrived = [lax.ppermute(value, "blk", [(i, i ^ m) for i in range(size)]) for m in masks]
        for other in arrived:
            value = combine(value, other)
        step *= 2 ** len(masks[:2])
    return value


def local(
    layer_input_tokens,
    input_norm_gain,
    query_weight,
    key_value_weight,
    output_weight,
    adapter_down_weight,
    adapter_up_weight,
    key_value_page_pool,
    request_adapter,
    adapter_storage_slot,
    cached_lengths,
    request_page_tables,
):
    own_index = lax.axis_index("blk")
    gathered = lax.all_gather(layer_input_tokens, "blk", axis=1, tiled=True)
    normalized_input = normalize(gathered, input_norm_gain)
    request_count = cached_lengths.shape[0]
    adapter_total = adapter_storage_slot.shape[0]
    choose = request_adapter[:, None] == jnp.arange(adapter_total, dtype=jnp.int32)[None, :]
    req_slot = jnp.sum(jnp.where(choose, adapter_storage_slot[None, :], 0), axis=1)
    token_cache_slot = jnp.repeat(req_slot, NEW_TOKENS)
    local_token_count = adapter_down_weight.shape[0]
    local_pick = (
        token_cache_slot[:, None] - own_index * local_token_count
        == jnp.arange(local_token_count, dtype=jnp.int32)[None, :]
    )
    output_projected = jnp.einsum(
        "ly,mxy->lmx", normalized_input, adapter_down_weight, preferred_element_type=jnp.float32
    )
    partial_codes = jnp.sum(jnp.where(local_pick[:, :, None], output_projected, 0.0), axis=1)
    adapter_choice_index = butterfly(partial_codes.astype(jnp.bfloat16), jnp.add)
    slot_count, adapter_rank, _ = adapter_up_weight.shape
    slot_pick = token_cache_slot[:, None] == jnp.arange(slot_count, dtype=jnp.int32)[None, :]
    spread_codes = jnp.where(
        slot_pick[:, :, None], adapter_choice_index[:, None, :], jnp.zeros((), jnp.bfloat16)
    ).reshape(token_cache_slot.shape[0], slot_count * adapter_rank)
    adapter_query_update = jnp.dot(
        spread_codes,
        adapter_up_weight.reshape(slot_count * adapter_rank, -1),
        preferred_element_type=jnp.float32,
    )
    token_positions = positions_of(cached_lengths)
    query_cols = query_weight.shape[1]
    keyval_cols = key_value_weight.shape[1]
    both_parts = jnp.concatenate(
        [
            jnp.dot(normalized_input, query_weight, preferred_element_type=jnp.float32)
            + adapter_query_update,
            jnp.dot(normalized_input, key_value_weight, preferred_element_type=jnp.float32),
        ],
        axis=1,
    )
    global_cols = jnp.concatenate(
        [
            own_index * query_cols + jnp.arange(query_cols, dtype=jnp.int32),
            own_index * keyval_cols + jnp.arange(keyval_cols, dtype=jnp.int32),
        ]
    )
    limits = jnp.concatenate(
        [
            jnp.full((query_cols,), QUERY_HEADS * HEAD_WIDTH, jnp.int32),
            jnp.full((keyval_cols,), KEY_VALUE_HEADS * HEAD_WIDTH, jnp.int32),
        ]
    )
    rotated_parts = rotate_columns(both_parts, token_positions, global_cols, limits)
    joined = lax.all_gather(rotated_parts, "blk", axis=1, tiled=False)
    query_vectors = joined[:, :, :query_cols].reshape(joined.shape[0], -1)
    key_value_rows = joined[:, :, query_cols:].reshape(joined.shape[0], -1)
    query_group_width = QUERY_HEADS // KEY_VALUE_HEADS
    query_feature_width = query_group_width * NEW_TOKENS
    score_scale = 1.0 / math.sqrt(HEAD_WIDTH)
    query_split = query_vectors.reshape(
        request_count, NEW_TOKENS, KEY_VALUE_HEADS, query_group_width, HEAD_WIDTH
    )
    fresh_token_rows = key_value_rows.reshape(
        request_count, NEW_TOKENS, 2, KEY_VALUE_HEADS, HEAD_WIDTH
    )
    request_page_count = key_value_page_pool.shape[0]
    table_width = request_page_tables.shape[1]
    page_ids = own_index * request_page_count + jnp.arange(request_page_count, dtype=jnp.int32)
    matches = request_page_tables[None, :, :] == page_ids[:, None, None]
    page_owner = jnp.any(matches, axis=2)
    page_live = jnp.any(page_owner, axis=1)
    page_req = jnp.sum(
        jnp.where(page_owner, jnp.arange(request_count, dtype=jnp.int32)[None, :], 0), axis=1
    )
    page_slot = jnp.sum(
        jnp.where(matches, jnp.arange(table_width, dtype=jnp.int32)[None, None, :], 0), axis=(1, 2)
    )
    page_len = jnp.sum(jnp.where(page_owner, cached_lengths[None, :], 0), axis=1)
    key_pos = page_slot[:, None] * PAGE_LENGTH + jnp.arange(PAGE_LENGTH, dtype=jnp.int32)[None, :]
    key_valid = page_live[:, None] & (key_pos < page_len[:, None])
    valid_full = key_valid[:, None, None, :]
    gathered_cache_pages = key_value_page_pool.reshape(
        request_page_count, PAGE_LENGTH, 2, KEY_VALUE_HEADS, HEAD_WIDTH
    )
    query_page = (
        query_split[page_req]
        .transpose(0, 2, 1, 3, 4)
        .reshape(request_page_count, KEY_VALUE_HEADS, query_feature_width, HEAD_WIDTH)
    )
    scores = (
        jnp.einsum(
            "skqd,spkd->skqp",
            query_page,
            gathered_cache_pages[:, :, 0],
            preferred_element_type=jnp.float32,
        )
        * score_scale
    )
    masked = jnp.where(valid_full, scores, neg_large)
    page_peak = jnp.max(masked, axis=-1)
    req_peak = jnp.max(
        jnp.where(page_owner[:, :, None, None], page_peak[:, None], neg_large), axis=0
    )
    query_wide = query_split.astype(jnp.float32)
    fresh_keys = fresh_token_rows[:, :, 0].astype(jnp.float32)
    fresh_scores = (
        jnp.stack(
            [
                jnp.sum(query_wide * fresh_keys[:, j][:, None, :, None, :], axis=-1)
                for j in range(NEW_TOKENS)
            ],
            axis=-1,
        )
        .transpose(0, 2, 1, 3, 4)
        .reshape(request_count, KEY_VALUE_HEADS, query_feature_width, NEW_TOKENS)
        * score_scale
    )
    step_of = jnp.arange(query_feature_width, dtype=jnp.int32) // query_group_width
    fresh_ok = (jnp.arange(NEW_TOKENS, dtype=jnp.int32)[None, :] <= step_of[:, None])[None, None]
    fresh_masked = jnp.where(fresh_ok, fresh_scores, neg_large)
    top_score = butterfly(jnp.maximum(req_peak, jnp.max(fresh_masked, axis=-1)), jnp.maximum)
    weights = jnp.where(valid_full, jnp.exp(masked - top_score[page_req][..., None]), 0.0)
    page_num = jnp.einsum(
        "skqp,spkd->skqd",
        weights.astype(jnp.bfloat16),
        gathered_cache_pages[:, :, 1],
        preferred_element_type=jnp.float32,
    )
    device_count = lax.axis_size("blk")
    head_count = QUERY_HEADS
    owner_cols = query_cols
    owner_heads = max(1, owner_cols // HEAD_WIDTH)
    head_repeat = min(owner_cols, HEAD_WIDTH)
    owner_first_head = [(o * owner_cols) // HEAD_WIDTH for o in range(device_count)]
    head_pick = jnp.asarray(
        [[first + j for j in range(owner_heads)] for first in owner_first_head], jnp.int32
    )
    slot_num = to_tokens(page_num).reshape(request_page_count, NEW_TOKENS, device_count, owner_cols)
    slot_den = to_tokens(jnp.sum(weights, axis=-1)[..., None]).reshape(
        request_page_count, NEW_TOKENS, head_count
    )
    slot_den_owner = slot_den[:, :, head_pick]
    packed = jnp.concatenate([slot_num, slot_den_owner], axis=3).transpose(2, 0, 1, 3)
    received = lax.all_to_all(packed, "blk", 0, 0, tiled=True)
    group_pages = device_count * request_page_count
    all_page_ids = jnp.arange(group_pages, dtype=jnp.int32)
    all_owner = jnp.any(request_page_tables[None, :, :] == all_page_ids[:, None, None], axis=2)
    pick_req = all_owner.T.astype(jnp.float32)
    summed = jnp.einsum(
        "rp,px->rx",
        pick_req,
        received.reshape(group_pages, -1),
        precision=lax.Precision.HIGHEST,
    ).reshape(request_count, NEW_TOKENS, owner_cols + owner_heads)
    fresh_weights = jnp.where(fresh_ok, jnp.exp(fresh_masked - top_score[..., None]), 0.0)
    fresh_by_head = (
        fresh_weights.reshape(
            request_count, KEY_VALUE_HEADS, NEW_TOKENS, query_group_width, NEW_TOKENS
        )
        .transpose(0, 2, 1, 3, 4)
        .reshape(request_count, NEW_TOKENS, QUERY_HEADS, NEW_TOKENS)
    )
    first_head = (own_index * owner_cols) // HEAD_WIDTH
    weights_own = lax.dynamic_slice_in_dim(fresh_by_head, first_head, owner_heads, axis=2)
    value_col = (
        KEY_VALUE_HEADS * HEAD_WIDTH
        + (first_head // query_group_width) * HEAD_WIDTH
        + (own_index * owner_cols) % HEAD_WIDTH
    )
    values_own = lax.dynamic_slice_in_dim(
        key_value_rows.reshape(request_count, NEW_TOKENS, -1), value_col, head_repeat, axis=2
    )
    fresh_num_own = jnp.einsum(
        "rihj,rjd->rihd",
        weights_own.astype(jnp.bfloat16),
        values_own,
        preferred_element_type=jnp.float32,
    ).reshape(request_count * NEW_TOKENS, owner_cols)
    fresh_den_own = jnp.sum(weights_own, axis=-1).reshape(request_count * NEW_TOKENS, owner_heads)
    num_own = summed[:, :, :owner_cols].reshape(request_count * NEW_TOKENS, owner_cols)
    den_own = summed[:, :, owner_cols:].reshape(request_count * NEW_TOKENS, owner_heads)
    totals = den_own + fresh_den_own
    attended_own = ((num_own + fresh_num_own) / jnp.repeat(totals, head_repeat, axis=1)).astype(
        jnp.bfloat16
    )
    attended = lax.all_gather(attended_own, "blk", axis=1, tiled=True)
    return jnp.dot(attended, output_weight, preferred_element_type=jnp.float32).astype(jnp.bfloat16)


def solution(mesh):
    placed = (
        P("groups", "blk"),
        P(),
        P(None, "blk"),
        P(None, "blk"),
        P(None, "blk"),
        P("blk", None, None),
        P(None, None, "blk"),
        P(("groups", "blk"), None, None),
        P("groups"),
        P(),
        P("groups"),
        P("groups", None),
    )
    return jax.shard_map(
        local, mesh=mesh, in_specs=placed, out_specs=P("groups", "blk"), check_vma=False
    )
```

```python
import math

import jax
import jax.numpy as jnp
from jax import lax
from jax.experimental import pallas as pl
from jax.experimental.pallas import tpu as pltpu
from jax.sharding import PartitionSpec as P

QUERY_HEADS = 64
KEY_VALUE_HEADS = 8
HEAD_WIDTH = 128
PAGE_LENGTH = 128
NEW_TOKENS = 3


theta_base = 500000.0
neg_large = -1e30


def apply_rotation(values, token_positions, first_col, rot_limit):
    width_cols = values.shape[1]
    columns = first_col + jnp.arange(width_cols, dtype=jnp.int32)
    pair_index = (columns % HEAD_WIDTH // 2).astype(jnp.float32)
    inverse = jnp.exp(pair_index * (-2.0 * math.log(theta_base) / HEAD_WIDTH))
    angles = token_positions[:, None] * inverse[None, :]
    cos_val = jnp.cos(angles[:, 0::2])
    sine_val = jnp.sin(angles[:, 0::2])
    even_part = values[:, 0::2]
    odd_part = values[:, 1::2]
    turned = jnp.stack(
        [even_part * cos_val - odd_part * sine_val, even_part * sine_val + odd_part * cos_val],
        axis=-1,
    ).reshape(values.shape)
    return jnp.where((columns < rot_limit)[None, :], turned, values)


def rotation_kernel(values_ref, cos_ref, sine_ref, out_ref):
    values = values_ref[...]
    width = values.shape[1]
    following = pltpu.roll(values, width - 1, 1)
    preceding = pltpu.roll(values, 1, 1)
    even = lax.broadcasted_iota(jnp.int32, values.shape, 1) % 2 == 0
    cos_val = cos_ref[...]
    sine_val = sine_ref[...]
    out_ref[...] = jnp.where(
        even, values * cos_val - following * sine_val, preceding * sine_val + values * cos_val
    ).astype(out_ref.dtype)


def rotate_columns(values, token_positions, global_cols, rot_limit):
    pair_index = (global_cols % HEAD_WIDTH // 2).astype(jnp.float32)
    inverse = jnp.exp(pair_index * (-2.0 * math.log(theta_base) / HEAD_WIDTH))
    angles = token_positions[:, None] * inverse[None, :]
    rotated = (global_cols < rot_limit)[None, :]
    cos_val = jnp.where(rotated, jnp.cos(angles), 1.0)
    sine_val = jnp.where(rotated, jnp.sin(angles), 0.0)
    width = values.shape[1]
    pad = -(-width // 128) * 128 - width
    operands = [jnp.pad(a, ((0, 0), (0, pad))) for a in (values, cos_val, sine_val)]
    out = pl.pallas_call(
        rotation_kernel,
        out_shape=jax.ShapeDtypeStruct(operands[0].shape, jnp.bfloat16),
    )(*operands)
    return out[:, :width]


def normalize(layer_input_tokens, input_norm_gain):
    values = layer_input_tokens.astype(jnp.float32)
    mean_square = jnp.mean(values * values, axis=-1, keepdims=True)
    return (values * lax.rsqrt(mean_square + 1e-05) * input_norm_gain[None, :]).astype(jnp.bfloat16)


def positions_of(cached_lengths):
    steps_row = jnp.arange(NEW_TOKENS, dtype=jnp.int32)
    return (
        jnp.repeat(cached_lengths, NEW_TOKENS) + jnp.tile(steps_row, cached_lengths.shape[0])
    ).astype(jnp.float32)


def to_tokens(request_first_layout):
    request_count = request_first_layout.shape[0]
    trailing_shape = request_first_layout.shape[3:]
    query_group_width = QUERY_HEADS // KEY_VALUE_HEADS
    split_head_shape = request_first_layout.reshape(
        (request_count, KEY_VALUE_HEADS, NEW_TOKENS, query_group_width) + trailing_shape
    )
    order_axes = (0, 2, 1, 3) + tuple(range(4, 4 + len(trailing_shape)))
    return split_head_shape.transpose(order_axes).reshape(request_count * NEW_TOKENS, -1)


def butterfly(value, combine):
    size = lax.axis_size("blk")
    step = 1
    while step < size:
        masks = [step] if step * 2 >= size else [step, step * 2, step * 3]
        arrived = [lax.ppermute(value, "blk", [(i, i ^ m) for i in range(size)]) for m in masks]
        for other in arrived:
            value = combine(value, other)
        step *= 2 ** len(masks[:2])
    return value


def local(
    layer_input_tokens,
    input_norm_gain,
    query_weight,
    key_value_weight,
    output_weight,
    adapter_down_weight,
    adapter_up_weight,
    key_value_page_pool,
    request_adapter,
    adapter_storage_slot,
    cached_lengths,
    request_page_tables,
):
    own_index = lax.axis_index("blk")
    gathered = lax.all_gather(layer_input_tokens, "blk", axis=1, tiled=True)
    normalized_input = normalize(gathered, input_norm_gain)
    request_count = cached_lengths.shape[0]
    adapter_total = adapter_storage_slot.shape[0]
    choose = request_adapter[:, None] == jnp.arange(adapter_total, dtype=jnp.int32)[None, :]
    req_slot = jnp.sum(jnp.where(choose, adapter_storage_slot[None, :], 0), axis=1)
    token_cache_slot = jnp.repeat(req_slot, NEW_TOKENS)
    local_token_count = adapter_down_weight.shape[0]
    local_pick = (
        token_cache_slot[:, None] - own_index * local_token_count
        == jnp.arange(local_token_count, dtype=jnp.int32)[None, :]
    )
    output_projected = jnp.einsum(
        "ly,mxy->lmx", normalized_input, adapter_down_weight, preferred_element_type=jnp.float32
    )
    partial_codes = jnp.sum(jnp.where(local_pick[:, :, None], output_projected, 0.0), axis=1)
    adapter_choice_index = butterfly(partial_codes.astype(jnp.bfloat16), jnp.add)
    slot_count, adapter_rank, _ = adapter_up_weight.shape
    slot_pick = token_cache_slot[:, None] == jnp.arange(slot_count, dtype=jnp.int32)[None, :]
    spread_codes = jnp.where(
        slot_pick[:, :, None], adapter_choice_index[:, None, :], jnp.zeros((), jnp.bfloat16)
    ).reshape(token_cache_slot.shape[0], slot_count * adapter_rank)
    adapter_query_update = jnp.dot(
        spread_codes,
        adapter_up_weight.reshape(slot_count * adapter_rank, -1),
        preferred_element_type=jnp.float32,
    )
    token_positions = positions_of(cached_lengths)
    query_cols = query_weight.shape[1]
    keyval_cols = key_value_weight.shape[1]
    both_parts = jnp.concatenate(
        [
            jnp.dot(normalized_input, query_weight, preferred_element_type=jnp.float32)
            + adapter_query_update,
            jnp.dot(normalized_input, key_value_weight, preferred_element_type=jnp.float32),
        ],
        axis=1,
    )
    global_cols = jnp.concatenate(
        [
            own_index * query_cols + jnp.arange(query_cols, dtype=jnp.int32),
            own_index * keyval_cols + jnp.arange(keyval_cols, dtype=jnp.int32),
        ]
    )
    limits = jnp.concatenate(
        [
            jnp.full((query_cols,), QUERY_HEADS * HEAD_WIDTH, jnp.int32),
            jnp.full((keyval_cols,), KEY_VALUE_HEADS * HEAD_WIDTH, jnp.int32),
        ]
    )
    rotated_parts = rotate_columns(both_parts, token_positions, global_cols, limits)
    joined = lax.all_gather(rotated_parts, "blk", axis=1, tiled=False)
    query_vectors = joined[:, :, :query_cols].reshape(joined.shape[0], -1)
    key_value_rows = joined[:, :, query_cols:].reshape(joined.shape[0], -1)
    query_group_width = QUERY_HEADS // KEY_VALUE_HEADS
    query_feature_width = query_group_width * NEW_TOKENS
    score_scale = 1.0 / math.sqrt(HEAD_WIDTH)
    query_split = query_vectors.reshape(
        request_count, NEW_TOKENS, KEY_VALUE_HEADS, query_group_width, HEAD_WIDTH
    )
    fresh_token_rows = key_value_rows.reshape(
        request_count, NEW_TOKENS, 2, KEY_VALUE_HEADS, HEAD_WIDTH
    )
    request_page_count = key_value_page_pool.shape[0]
    table_width = request_page_tables.shape[1]
    page_ids = own_index * request_page_count + jnp.arange(request_page_count, dtype=jnp.int32)
    matches = request_page_tables[None, :, :] == page_ids[:, None, None]
    page_owner = jnp.any(matches, axis=2)
    page_live = jnp.any(page_owner, axis=1)
    page_req = jnp.sum(
        jnp.where(page_owner, jnp.arange(request_count, dtype=jnp.int32)[None, :], 0), axis=1
    )
    page_slot = jnp.sum(
        jnp.where(matches, jnp.arange(table_width, dtype=jnp.int32)[None, None, :], 0), axis=(1, 2)
    )
    page_len = jnp.sum(jnp.where(page_owner, cached_lengths[None, :], 0), axis=1)
    key_pos = page_slot[:, None] * PAGE_LENGTH + jnp.arange(PAGE_LENGTH, dtype=jnp.int32)[None, :]
    key_valid = page_live[:, None] & (key_pos < page_len[:, None])
    valid_full = key_valid[:, None, None, :]
    gathered_cache_pages = key_value_page_pool.reshape(
        request_page_count, PAGE_LENGTH, 2, KEY_VALUE_HEADS, HEAD_WIDTH
    )
    query_page = (
        query_split[page_req]
        .transpose(0, 2, 1, 3, 4)
        .reshape(request_page_count, KEY_VALUE_HEADS, query_feature_width, HEAD_WIDTH)
    )
    scores = (
        jnp.einsum(
            "skqd,spkd->skqp",
            query_page,
            gathered_cache_pages[:, :, 0],
            preferred_element_type=jnp.float32,
        )
        * score_scale
    )
    masked = jnp.where(valid_full, scores, neg_large)
    page_peak = jnp.max(masked, axis=-1)
    weights = jnp.where(valid_full, jnp.exp(masked - page_peak[..., None]), 0.0)
    page_num = jnp.einsum(
        "skqp,spkd->skqd",
        weights.astype(jnp.bfloat16),
        gathered_cache_pages[:, :, 1],
        preferred_element_type=jnp.float32,
    )
    device_count = lax.axis_size("blk")
    head_count = QUERY_HEADS
    owner_cols = query_cols
    owner_heads = max(1, owner_cols // HEAD_WIDTH)
    head_repeat = min(owner_cols, HEAD_WIDTH)
    owner_first_head = [(o * owner_cols) // HEAD_WIDTH for o in range(device_count)]
    head_pick = jnp.asarray(
        [[first + j for j in range(owner_heads)] for first in owner_first_head], jnp.int32
    )
    slot_num = to_tokens(page_num).reshape(request_page_count, NEW_TOKENS, device_count, owner_cols)
    slot_den = to_tokens(jnp.sum(weights, axis=-1)[..., None]).reshape(
        request_page_count, NEW_TOKENS, head_count
    )
    slot_peak = to_tokens(page_peak[..., None]).reshape(request_page_count, NEW_TOKENS, head_count)
    packed = jnp.concatenate(
        [
            part.transpose(2, 0, 1, 3).reshape(device_count, request_page_count, -1)
            for part in (slot_num, slot_den[:, :, head_pick], slot_peak[:, :, head_pick])
        ],
        axis=2,
    )
    received = lax.all_to_all(packed, "blk", 0, 0, tiled=True)
    group_pages = device_count * request_page_count
    listed_pages = request_page_tables.reshape(-1)
    listed_target = jnp.where(listed_pages >= 0, listed_pages, group_pages)
    page_of_req = (
        jnp.zeros((group_pages,), jnp.int32)
        .at[listed_target]
        .set(jnp.repeat(jnp.arange(request_count, dtype=jnp.int32), table_width), mode="drop")
    )
    page_used = jnp.zeros((group_pages,), jnp.bool_).at[listed_target].set(True, mode="drop")
    owner_of_page = (
        jnp.arange(request_count, dtype=jnp.int32)[:, None] == page_of_req[None, :]
    ) & page_used[None, :]
    arrived = received.reshape(group_pages, -1)
    num_width = NEW_TOKENS * owner_cols
    head_width = NEW_TOKENS * owner_heads
    arrived_num = arrived[:, :num_width]
    arrived_den = arrived[:, num_width : num_width + head_width]
    arrived_peak = arrived[:, num_width + head_width :]
    first_head = (own_index * owner_cols) // HEAD_WIDTH
    kv_head = first_head // query_group_width
    query_own = lax.dynamic_slice_in_dim(
        query_vectors.reshape(request_count, NEW_TOKENS, QUERY_HEADS, HEAD_WIDTH),
        first_head,
        owner_heads,
        axis=2,
    )
    fresh_rows = key_value_rows.reshape(request_count, NEW_TOKENS, -1)
    keys_own = lax.dynamic_slice_in_dim(fresh_rows, kv_head * HEAD_WIDTH, HEAD_WIDTH, axis=2)
    fresh_scores = (
        jnp.einsum("rihd,rjd->rihj", query_own, keys_own, preferred_element_type=jnp.float32)
        * score_scale
    )
    causal = (jnp.arange(NEW_TOKENS)[None, :] <= jnp.arange(NEW_TOKENS)[:, None])[None, :, None, :]
    fresh_masked = jnp.where(causal, fresh_scores, neg_large)
    slot_best = jnp.max(
        jnp.where(owner_of_page[:, None, :], arrived_peak.T[None], neg_large), axis=2
    )
    top_flat = jnp.maximum(slot_best, jnp.max(fresh_masked, axis=-1).reshape(request_count, -1))
    top_score = top_flat.reshape(request_count, NEW_TOKENS, owner_heads)
    rescale = jnp.exp(arrived_peak - top_flat[page_of_req])
    rescaled = jnp.concatenate(
        [arrived_num * jnp.repeat(rescale, head_repeat, axis=1), arrived_den * rescale], axis=1
    )
    pick_req = owner_of_page.astype(jnp.float32)
    summed = jnp.einsum("rp,px->rx", pick_req, rescaled, precision=lax.Precision.HIGHEST)
    weights_own = jnp.where(causal, jnp.exp(fresh_masked - top_score[..., None]), 0.0)
    value_col = (
        KEY_VALUE_HEADS * HEAD_WIDTH + kv_head * HEAD_WIDTH + (own_index * owner_cols) % HEAD_WIDTH
    )
    values_own = lax.dynamic_slice_in_dim(fresh_rows, value_col, head_repeat, axis=2)
    fresh_num_own = jnp.einsum(
        "rihj,rjd->rihd",
        weights_own.astype(jnp.bfloat16),
        values_own,
        preferred_element_type=jnp.float32,
    ).reshape(request_count * NEW_TOKENS, owner_cols)
    fresh_den_own = jnp.sum(weights_own, axis=-1).reshape(request_count * NEW_TOKENS, owner_heads)
    num_own = summed[:, :num_width].reshape(request_count * NEW_TOKENS, owner_cols)
    den_own = summed[:, num_width:].reshape(request_count * NEW_TOKENS, owner_heads)
    totals = den_own + fresh_den_own
    attended_own = ((num_own + fresh_num_own) / jnp.repeat(totals, head_repeat, axis=1)).astype(
        jnp.bfloat16
    )
    attended = lax.all_gather(attended_own, "blk", axis=1, tiled=True)
    return jnp.dot(attended, output_weight, preferred_element_type=jnp.float32).astype(jnp.bfloat16)


def solution(mesh):
    placed = (
        P("groups", "blk"),
        P(),
        P(None, "blk"),
        P(None, "blk"),
        P(None, "blk"),
        P("blk", None, None),
        P(None, None, "blk"),
        P(("groups", "blk"), None, None),
        P("groups"),
        P(),
        P("groups"),
        P("groups", None),
    )
    return jax.shard_map(
        local, mesh=mesh, in_specs=placed, out_specs=P("groups", "blk"), check_vma=False
    )
```

```python
import math

import jax
import jax.numpy as jnp
from jax import lax
from jax.experimental import pallas as pl
from jax.experimental.pallas import tpu as pltpu
from jax.sharding import PartitionSpec as P

QUERY_HEADS = 64
KEY_VALUE_HEADS = 8
HEAD_WIDTH = 128
PAGE_LENGTH = 128
NEW_TOKENS = 3


theta_base = 500000.0
neg_large = -1e30


def apply_rotation(values, token_positions, first_col, rot_limit):
    width_cols = values.shape[1]
    columns = first_col + jnp.arange(width_cols, dtype=jnp.int32)
    pair_index = (columns % HEAD_WIDTH // 2).astype(jnp.float32)
    inverse = jnp.exp(pair_index * (-2.0 * math.log(theta_base) / HEAD_WIDTH))
    angles = token_positions[:, None] * inverse[None, :]
    cos_val = jnp.cos(angles[:, 0::2])
    sine_val = jnp.sin(angles[:, 0::2])
    even_part = values[:, 0::2]
    odd_part = values[:, 1::2]
    turned = jnp.stack(
        [even_part * cos_val - odd_part * sine_val, even_part * sine_val + odd_part * cos_val],
        axis=-1,
    ).reshape(values.shape)
    return jnp.where((columns < rot_limit)[None, :], turned, values)


def rotation_kernel(values_ref, cos_ref, sine_ref, out_ref):
    values = values_ref[...]
    width = values.shape[1]
    following = pltpu.roll(values, width - 1, 1)
    preceding = pltpu.roll(values, 1, 1)
    even = lax.broadcasted_iota(jnp.int32, values.shape, 1) % 2 == 0
    cos_val = cos_ref[...]
    sine_val = sine_ref[...]
    out_ref[...] = jnp.where(
        even, values * cos_val - following * sine_val, preceding * sine_val + values * cos_val
    ).astype(out_ref.dtype)


def rotate_columns(values, token_positions, global_cols, rot_limit):
    pair_index = (global_cols % HEAD_WIDTH // 2).astype(jnp.float32)
    inverse = jnp.exp(pair_index * (-2.0 * math.log(theta_base) / HEAD_WIDTH))
    angles = token_positions[:, None] * inverse[None, :]
    rotated = (global_cols < rot_limit)[None, :]
    cos_val = jnp.where(rotated, jnp.cos(angles), 1.0)
    sine_val = jnp.where(rotated, jnp.sin(angles), 0.0)
    width = values.shape[1]
    pad = -(-width // 128) * 128 - width
    operands = [jnp.pad(a, ((0, 0), (0, pad))) for a in (values, cos_val, sine_val)]
    out = pl.pallas_call(
        rotation_kernel,
        out_shape=jax.ShapeDtypeStruct(operands[0].shape, jnp.bfloat16),
    )(*operands)
    return out[:, :width]


def normalize(layer_input_tokens, input_norm_gain):
    values = layer_input_tokens.astype(jnp.float32)
    mean_square = jnp.mean(values * values, axis=-1, keepdims=True)
    return (values * lax.rsqrt(mean_square + 1e-05) * input_norm_gain[None, :]).astype(jnp.bfloat16)


def positions_of(cached_lengths):
    steps_row = jnp.arange(NEW_TOKENS, dtype=jnp.int32)
    return (
        jnp.repeat(cached_lengths, NEW_TOKENS) + jnp.tile(steps_row, cached_lengths.shape[0])
    ).astype(jnp.float32)


def to_tokens(request_first_layout):
    request_count = request_first_layout.shape[0]
    trailing_shape = request_first_layout.shape[3:]
    query_group_width = QUERY_HEADS // KEY_VALUE_HEADS
    split_head_shape = request_first_layout.reshape(
        (request_count, KEY_VALUE_HEADS, NEW_TOKENS, query_group_width) + trailing_shape
    )
    order_axes = (0, 2, 1, 3) + tuple(range(4, 4 + len(trailing_shape)))
    return split_head_shape.transpose(order_axes).reshape(request_count * NEW_TOKENS, -1)


def butterfly(value, combine):
    size = lax.axis_size("blk")
    step = 1
    while step < size:
        masks = [step] if step * 2 >= size else [step, step * 2, step * 3]
        arrived = [lax.ppermute(value, "blk", [(i, i ^ m) for i in range(size)]) for m in masks]
        for other in arrived:
            value = combine(value, other)
        step *= 2 ** len(masks[:2])
    return value


def local(
    layer_input_tokens,
    input_norm_gain,
    query_weight,
    key_value_weight,
    output_weight,
    adapter_down_weight,
    adapter_up_weight,
    key_value_page_pool,
    request_adapter,
    adapter_storage_slot,
    cached_lengths,
    request_page_tables,
):
    own_index = lax.axis_index("blk")
    gathered = lax.all_gather(layer_input_tokens, "blk", axis=1, tiled=True)
    normalized_input = normalize(gathered, input_norm_gain)
    request_count = cached_lengths.shape[0]
    adapter_total = adapter_storage_slot.shape[0]
    choose = request_adapter[:, None] == jnp.arange(adapter_total, dtype=jnp.int32)[None, :]
    req_slot = jnp.sum(jnp.where(choose, adapter_storage_slot[None, :], 0), axis=1)
    token_cache_slot = jnp.repeat(req_slot, NEW_TOKENS)
    local_token_count = adapter_down_weight.shape[0]
    local_pick = (
        token_cache_slot[:, None] - own_index * local_token_count
        == jnp.arange(local_token_count, dtype=jnp.int32)[None, :]
    )
    output_projected = jnp.einsum(
        "ly,mxy->lmx", normalized_input, adapter_down_weight, preferred_element_type=jnp.float32
    )
    partial_codes = jnp.sum(jnp.where(local_pick[:, :, None], output_projected, 0.0), axis=1)
    adapter_choice_index = butterfly(partial_codes.astype(jnp.bfloat16), jnp.add)
    slot_count, adapter_rank, _ = adapter_up_weight.shape
    slot_pick = token_cache_slot[:, None] == jnp.arange(slot_count, dtype=jnp.int32)[None, :]
    spread_codes = jnp.where(
        slot_pick[:, :, None], adapter_choice_index[:, None, :], jnp.zeros((), jnp.bfloat16)
    ).reshape(token_cache_slot.shape[0], slot_count * adapter_rank)
    adapter_query_update = jnp.dot(
        spread_codes,
        adapter_up_weight.reshape(slot_count * adapter_rank, -1),
        preferred_element_type=jnp.float32,
    )
    token_positions = positions_of(cached_lengths)
    query_cols = query_weight.shape[1]
    keyval_cols = key_value_weight.shape[1]
    both_parts = jnp.concatenate(
        [
            jnp.dot(normalized_input, query_weight, preferred_element_type=jnp.float32)
            + adapter_query_update,
            jnp.dot(normalized_input, key_value_weight, preferred_element_type=jnp.float32),
        ],
        axis=1,
    )
    global_cols = jnp.concatenate(
        [
            own_index * query_cols + jnp.arange(query_cols, dtype=jnp.int32),
            own_index * keyval_cols + jnp.arange(keyval_cols, dtype=jnp.int32),
        ]
    )
    limits = jnp.concatenate(
        [
            jnp.full((query_cols,), QUERY_HEADS * HEAD_WIDTH, jnp.int32),
            jnp.full((keyval_cols,), KEY_VALUE_HEADS * HEAD_WIDTH, jnp.int32),
        ]
    )
    rotated_parts = rotate_columns(both_parts, token_positions, global_cols, limits)
    device_count = lax.axis_size("blk")
    request_page_count = key_value_page_pool.shape[0]
    table_width = request_page_tables.shape[1]
    group_pages = device_count * request_page_count
    listed_pages = request_page_tables.reshape(-1)
    listed_target = jnp.where(listed_pages >= 0, listed_pages, group_pages)
    page_of_req = (
        jnp.zeros((group_pages,), jnp.int32)
        .at[listed_target]
        .set(jnp.repeat(jnp.arange(request_count, dtype=jnp.int32), table_width), mode="drop")
    )
    page_used = jnp.zeros((group_pages,), jnp.bool_).at[listed_target].set(True, mode="drop")
    owner_of_page = (
        jnp.arange(request_count, dtype=jnp.int32)[:, None] == page_of_req[None, :]
    ) & page_used[None, :]
    part_rows = rotated_parts.reshape(request_count, NEW_TOKENS, -1)
    part_width = part_rows.shape[2]
    outgoing = part_rows[page_of_req].reshape(
        device_count, request_page_count, NEW_TOKENS * part_width
    )
    incoming = (
        lax.all_to_all(outgoing, "blk", 0, 0, tiled=True)
        .reshape(device_count, request_page_count, NEW_TOKENS, part_width)
        .transpose(1, 2, 0, 3)
    )
    slot_queries = incoming[..., :query_cols].reshape(request_page_count, NEW_TOKENS, -1)
    slot_fresh = incoming[..., query_cols:].reshape(
        request_page_count, NEW_TOKENS, 2, KEY_VALUE_HEADS, HEAD_WIDTH
    )
    query_group_width = QUERY_HEADS // KEY_VALUE_HEADS
    query_feature_width = query_group_width * NEW_TOKENS
    score_scale = 1.0 / math.sqrt(HEAD_WIDTH)
    page_ids = own_index * request_page_count + jnp.arange(request_page_count, dtype=jnp.int32)
    matches = request_page_tables[None, :, :] == page_ids[:, None, None]
    page_owner = jnp.any(matches, axis=2)
    page_live = jnp.any(page_owner, axis=1)
    page_slot = jnp.sum(
        jnp.where(matches, jnp.arange(table_width, dtype=jnp.int32)[None, None, :], 0), axis=(1, 2)
    )
    page_len = jnp.sum(jnp.where(page_owner, cached_lengths[None, :], 0), axis=1)
    key_pos = page_slot[:, None] * PAGE_LENGTH + jnp.arange(PAGE_LENGTH, dtype=jnp.int32)[None, :]
    key_valid = page_live[:, None] & (key_pos < page_len[:, None])
    valid_full = key_valid[:, None, None, :]
    takes_fresh = page_live & (page_slot == 0)
    step_of = jnp.arange(query_feature_width, dtype=jnp.int32) // query_group_width
    fresh_valid = takes_fresh[:, None, None, None] & (
        jnp.arange(NEW_TOKENS, dtype=jnp.int32)[None, None, None, :] <= step_of[None, None, :, None]
    )
    cache_pages = key_value_page_pool.reshape(
        request_page_count, PAGE_LENGTH, 2, KEY_VALUE_HEADS, HEAD_WIDTH
    )
    query_page = (
        slot_queries.reshape(
            request_page_count, NEW_TOKENS, KEY_VALUE_HEADS, query_group_width, HEAD_WIDTH
        )
        .transpose(0, 2, 1, 3, 4)
        .reshape(request_page_count, KEY_VALUE_HEADS, query_feature_width, HEAD_WIDTH)
    )
    scores = (
        jnp.einsum(
            "skqd,spkd->skqp", query_page, cache_pages[:, :, 0], preferred_element_type=jnp.float32
        )
        * score_scale
    )
    fresh_scores = (
        jnp.einsum(
            "skqd,sjkd->skqj", query_page, slot_fresh[:, :, 0], preferred_element_type=jnp.float32
        )
        * score_scale
    )
    masked = jnp.where(valid_full, scores, neg_large)
    fresh_masked = jnp.where(fresh_valid, fresh_scores, neg_large)
    page_peak = jnp.maximum(jnp.max(masked, axis=-1), jnp.max(fresh_masked, axis=-1))
    weights = jnp.where(valid_full, jnp.exp(masked - page_peak[..., None]), 0.0)
    fresh_weights = jnp.where(fresh_valid, jnp.exp(fresh_masked - page_peak[..., None]), 0.0)
    page_num = jnp.einsum(
        "skqp,spkd->skqd",
        weights.astype(jnp.bfloat16),
        cache_pages[:, :, 1],
        preferred_element_type=jnp.float32,
    ) + jnp.einsum(
        "skqj,sjkd->skqd",
        fresh_weights.astype(jnp.bfloat16),
        slot_fresh[:, :, 1],
        preferred_element_type=jnp.float32,
    )
    page_den = jnp.sum(weights, axis=-1) + jnp.sum(fresh_weights, axis=-1)
    head_count = QUERY_HEADS
    owner_cols = query_cols
    owner_heads = max(1, owner_cols // HEAD_WIDTH)
    head_repeat = min(owner_cols, HEAD_WIDTH)
    owner_first_head = [(o * owner_cols) // HEAD_WIDTH for o in range(device_count)]
    head_pick = jnp.asarray(
        [[first + j for j in range(owner_heads)] for first in owner_first_head], jnp.int32
    )
    slot_num = to_tokens(page_num).reshape(request_page_count, NEW_TOKENS, device_count, owner_cols)
    slot_den = to_tokens(page_den[..., None]).reshape(request_page_count, NEW_TOKENS, head_count)
    slot_peak = to_tokens(page_peak[..., None]).reshape(request_page_count, NEW_TOKENS, head_count)
    packed = jnp.concatenate(
        [
            part.transpose(2, 0, 1, 3).reshape(device_count, request_page_count, -1)
            for part in (slot_num, slot_den[:, :, head_pick], slot_peak[:, :, head_pick])
        ],
        axis=2,
    )
    arrived = lax.all_to_all(packed, "blk", 0, 0, tiled=True).reshape(group_pages, -1)
    num_width = NEW_TOKENS * owner_cols
    head_width = NEW_TOKENS * owner_heads
    arrived_num = arrived[:, :num_width]
    arrived_den = arrived[:, num_width : num_width + head_width]
    arrived_peak = arrived[:, num_width + head_width :]
    top_flat = jnp.max(
        jnp.where(owner_of_page[:, None, :], arrived_peak.T[None], neg_large), axis=2
    )
    rescale = jnp.exp(arrived_peak - top_flat[page_of_req])
    rescaled = jnp.concatenate(
        [arrived_num * jnp.repeat(rescale, head_repeat, axis=1), arrived_den * rescale], axis=1
    )
    summed = jnp.einsum(
        "rp,px->rx", owner_of_page.astype(jnp.float32), rescaled, precision=lax.Precision.HIGHEST
    )
    num_own = summed[:, :num_width].reshape(request_count * NEW_TOKENS, owner_cols)
    den_own = summed[:, num_width:].reshape(request_count * NEW_TOKENS, owner_heads)
    attended_own = (num_own / jnp.repeat(den_own, head_repeat, axis=1)).astype(jnp.bfloat16)
    attended = lax.all_gather(attended_own, "blk", axis=1, tiled=True)
    return jnp.dot(attended, output_weight, preferred_element_type=jnp.float32).astype(jnp.bfloat16)


def solution(mesh):
    placed = (
        P("groups", "blk"),
        P(),
        P(None, "blk"),
        P(None, "blk"),
        P(None, "blk"),
        P("blk", None, None),
        P(None, None, "blk"),
        P(("groups", "blk"), None, None),
        P("groups"),
        P(),
        P("groups"),
        P("groups", None),
    )
    return jax.shard_map(
        local, mesh=mesh, in_specs=placed, out_specs=P("groups", "blk"), check_vma=False
    )
```

```python
import math

import jax
import jax.numpy as jnp
from jax import lax
from jax.experimental import pallas as pl
from jax.experimental.pallas import tpu as pltpu
from jax.sharding import PartitionSpec as P

QUERY_HEADS = 64
KEY_VALUE_HEADS = 8
HEAD_WIDTH = 128
PAGE_LENGTH = 128
NEW_TOKENS = 3


theta_base = 500000.0
neg_large = -1e30


def apply_rotation(values, token_positions, first_col, rot_limit):
    width_cols = values.shape[1]
    columns = first_col + jnp.arange(width_cols, dtype=jnp.int32)
    pair_index = (columns % HEAD_WIDTH // 2).astype(jnp.float32)
    inverse = jnp.exp(pair_index * (-2.0 * math.log(theta_base) / HEAD_WIDTH))
    angles = token_positions[:, None] * inverse[None, :]
    cos_val = jnp.cos(angles[:, 0::2])
    sine_val = jnp.sin(angles[:, 0::2])
    even_part = values[:, 0::2]
    odd_part = values[:, 1::2]
    turned = jnp.stack(
        [even_part * cos_val - odd_part * sine_val, even_part * sine_val + odd_part * cos_val],
        axis=-1,
    ).reshape(values.shape)
    return jnp.where((columns < rot_limit)[None, :], turned, values)


def rotation_kernel(values_ref, cos_ref, sine_ref, out_ref):
    values = values_ref[...]
    width = values.shape[1]
    following = pltpu.roll(values, width - 1, 1)
    preceding = pltpu.roll(values, 1, 1)
    even = lax.broadcasted_iota(jnp.int32, values.shape, 1) % 2 == 0
    cos_val = cos_ref[...]
    sine_val = sine_ref[...]
    out_ref[...] = jnp.where(
        even, values * cos_val - following * sine_val, preceding * sine_val + values * cos_val
    ).astype(out_ref.dtype)


def rotate_columns(values, token_positions, global_cols, rot_limit):
    pair_index = (global_cols % HEAD_WIDTH // 2).astype(jnp.float32)
    inverse = jnp.exp(pair_index * (-2.0 * math.log(theta_base) / HEAD_WIDTH))
    angles = token_positions[:, None] * inverse[None, :]
    rotated = (global_cols < rot_limit)[None, :]
    cos_val = jnp.where(rotated, jnp.cos(angles), 1.0)
    sine_val = jnp.where(rotated, jnp.sin(angles), 0.0)
    width = values.shape[1]
    pad = -(-width // 128) * 128 - width
    operands = [jnp.pad(a, ((0, 0), (0, pad))) for a in (values, cos_val, sine_val)]
    out = pl.pallas_call(
        rotation_kernel,
        out_shape=jax.ShapeDtypeStruct(operands[0].shape, jnp.bfloat16),
    )(*operands)
    return out[:, :width]


def normalize(layer_input_tokens, input_norm_gain):
    values = layer_input_tokens.astype(jnp.float32)
    mean_square = jnp.mean(values * values, axis=-1, keepdims=True)
    return (values * lax.rsqrt(mean_square + 1e-05) * input_norm_gain[None, :]).astype(jnp.bfloat16)


def positions_of(cached_lengths):
    steps_row = jnp.arange(NEW_TOKENS, dtype=jnp.int32)
    return (
        jnp.repeat(cached_lengths, NEW_TOKENS) + jnp.tile(steps_row, cached_lengths.shape[0])
    ).astype(jnp.float32)


def to_tokens(request_first_layout):
    request_count = request_first_layout.shape[0]
    trailing_shape = request_first_layout.shape[3:]
    query_group_width = QUERY_HEADS // KEY_VALUE_HEADS
    split_head_shape = request_first_layout.reshape(
        (request_count, KEY_VALUE_HEADS, NEW_TOKENS, query_group_width) + trailing_shape
    )
    order_axes = (0, 2, 1, 3) + tuple(range(4, 4 + len(trailing_shape)))
    return split_head_shape.transpose(order_axes).reshape(request_count * NEW_TOKENS, -1)


def butterfly(value, combine):
    size = lax.axis_size("blk")
    step = 1
    while step < size:
        masks = [step] if step * 2 >= size else [step, step * 2, step * 3]
        arrived = [lax.ppermute(value, "blk", [(i, i ^ m) for i in range(size)]) for m in masks]
        for other in arrived:
            value = combine(value, other)
        step *= 2 ** len(masks[:2])
    return value


def local(
    layer_input_tokens,
    input_norm_gain,
    query_weight,
    key_value_weight,
    output_weight,
    adapter_down_weight,
    adapter_up_weight,
    key_value_page_pool,
    request_adapter,
    adapter_storage_slot,
    cached_lengths,
    request_page_tables,
):
    own_index = lax.axis_index("blk")
    gathered = lax.all_gather(layer_input_tokens, "blk", axis=1, tiled=True)
    normalized_input = normalize(gathered, input_norm_gain)
    request_count = cached_lengths.shape[0]
    adapter_total = adapter_storage_slot.shape[0]
    choose = request_adapter[:, None] == jnp.arange(adapter_total, dtype=jnp.int32)[None, :]
    req_slot = jnp.sum(jnp.where(choose, adapter_storage_slot[None, :], 0), axis=1)
    token_cache_slot = jnp.repeat(req_slot, NEW_TOKENS)
    local_token_count = adapter_down_weight.shape[0]
    local_pick = (
        token_cache_slot[:, None] - own_index * local_token_count
        == jnp.arange(local_token_count, dtype=jnp.int32)[None, :]
    )
    output_projected = jnp.einsum(
        "ly,mxy->lmx", normalized_input, adapter_down_weight, preferred_element_type=jnp.float32
    )
    partial_codes = jnp.sum(jnp.where(local_pick[:, :, None], output_projected, 0.0), axis=1)
    adapter_choice_index = butterfly(partial_codes.astype(jnp.bfloat16), jnp.add)
    slot_count, adapter_rank, _ = adapter_up_weight.shape
    slot_pick = token_cache_slot[:, None] == jnp.arange(slot_count, dtype=jnp.int32)[None, :]
    spread_codes = jnp.where(
        slot_pick[:, :, None], adapter_choice_index[:, None, :], jnp.zeros((), jnp.bfloat16)
    ).reshape(token_cache_slot.shape[0], slot_count * adapter_rank)
    adapter_query_update = jnp.dot(
        spread_codes,
        adapter_up_weight.reshape(slot_count * adapter_rank, -1),
        preferred_element_type=jnp.float32,
    )
    token_positions = positions_of(cached_lengths)
    query_cols = query_weight.shape[1]
    keyval_cols = key_value_weight.shape[1]
    both_parts = jnp.concatenate(
        [
            jnp.dot(normalized_input, query_weight, preferred_element_type=jnp.float32)
            + adapter_query_update,
            jnp.dot(normalized_input, key_value_weight, preferred_element_type=jnp.float32),
        ],
        axis=1,
    )
    global_cols = jnp.concatenate(
        [
            own_index * query_cols + jnp.arange(query_cols, dtype=jnp.int32),
            own_index * keyval_cols + jnp.arange(keyval_cols, dtype=jnp.int32),
        ]
    )
    limits = jnp.concatenate(
        [
            jnp.full((query_cols,), QUERY_HEADS * HEAD_WIDTH, jnp.int32),
            jnp.full((keyval_cols,), KEY_VALUE_HEADS * HEAD_WIDTH, jnp.int32),
        ]
    )
    rotated_parts = rotate_columns(both_parts, token_positions, global_cols, limits)
    device_count = lax.axis_size("blk")
    request_page_count = key_value_page_pool.shape[0]
    table_width = request_page_tables.shape[1]
    group_pages = device_count * request_page_count
    listed_pages = request_page_tables.reshape(-1)
    listed_target = jnp.where(listed_pages >= 0, listed_pages, group_pages)
    page_of_req = (
        jnp.zeros((group_pages,), jnp.int32)
        .at[listed_target]
        .set(jnp.repeat(jnp.arange(request_count, dtype=jnp.int32), table_width), mode="drop")
    )
    page_used = jnp.zeros((group_pages,), jnp.bool_).at[listed_target].set(True, mode="drop")
    owner_of_page = (
        jnp.arange(request_count, dtype=jnp.int32)[:, None] == page_of_req[None, :]
    ) & page_used[None, :]
    part_rows = rotated_parts.reshape(request_count, NEW_TOKENS, -1)
    part_width = part_rows.shape[2]
    outgoing = part_rows[page_of_req].reshape(
        device_count, request_page_count, NEW_TOKENS * part_width
    )
    incoming = (
        lax.all_to_all(outgoing, "blk", 0, 0, tiled=True)
        .reshape(device_count, request_page_count, NEW_TOKENS, part_width)
        .transpose(1, 2, 0, 3)
    )
    slot_queries = incoming[..., :query_cols].reshape(request_page_count, NEW_TOKENS, -1)
    slot_fresh = incoming[..., query_cols:].reshape(
        request_page_count, NEW_TOKENS, 2, KEY_VALUE_HEADS, HEAD_WIDTH
    )
    query_group_width = QUERY_HEADS // KEY_VALUE_HEADS
    query_feature_width = query_group_width * NEW_TOKENS
    score_scale = 1.0 / math.sqrt(HEAD_WIDTH)
    page_ids = own_index * request_page_count + jnp.arange(request_page_count, dtype=jnp.int32)
    matches = request_page_tables[None, :, :] == page_ids[:, None, None]
    page_owner = jnp.any(matches, axis=2)
    page_live = jnp.any(page_owner, axis=1)
    page_slot = jnp.sum(
        jnp.where(matches, jnp.arange(table_width, dtype=jnp.int32)[None, None, :], 0), axis=(1, 2)
    )
    page_len = jnp.sum(jnp.where(page_owner, cached_lengths[None, :], 0), axis=1)
    key_pos = page_slot[:, None] * PAGE_LENGTH + jnp.arange(PAGE_LENGTH, dtype=jnp.int32)[None, :]
    key_valid = page_live[:, None] & (key_pos < page_len[:, None])
    valid_full = key_valid[:, None, None, :]
    takes_fresh = page_live & (page_slot == 0)
    step_of = jnp.arange(query_feature_width, dtype=jnp.int32) // query_group_width
    fresh_valid = takes_fresh[:, None, None, None] & (
        jnp.arange(NEW_TOKENS, dtype=jnp.int32)[None, None, None, :] <= step_of[None, None, :, None]
    )
    cache_pages = key_value_page_pool.reshape(
        request_page_count, PAGE_LENGTH, 2, KEY_VALUE_HEADS, HEAD_WIDTH
    )
    query_page = (
        slot_queries.reshape(
            request_page_count, NEW_TOKENS, KEY_VALUE_HEADS, query_group_width, HEAD_WIDTH
        )
        .transpose(0, 2, 1, 3, 4)
        .reshape(request_page_count, KEY_VALUE_HEADS, query_feature_width, HEAD_WIDTH)
    )
    scores = (
        jnp.einsum(
            "skqd,spkd->skqp", query_page, cache_pages[:, :, 0], preferred_element_type=jnp.float32
        )
        * score_scale
    )
    fresh_scores = (
        jnp.einsum(
            "skqd,sjkd->skqj", query_page, slot_fresh[:, :, 0], preferred_element_type=jnp.float32
        )
        * score_scale
    )
    masked = jnp.where(valid_full, scores, neg_large)
    fresh_masked = jnp.where(fresh_valid, fresh_scores, neg_large)
    page_peak = jnp.maximum(jnp.max(masked, axis=-1), jnp.max(fresh_masked, axis=-1))
    weights = jnp.where(valid_full, jnp.exp(masked - page_peak[..., None]), 0.0)
    fresh_weights = jnp.where(fresh_valid, jnp.exp(fresh_masked - page_peak[..., None]), 0.0)
    page_num = jnp.einsum(
        "skqp,spkd->skqd",
        weights.astype(jnp.bfloat16),
        cache_pages[:, :, 1],
        preferred_element_type=jnp.float32,
    ) + jnp.einsum(
        "skqj,sjkd->skqd",
        fresh_weights.astype(jnp.bfloat16),
        slot_fresh[:, :, 1],
        preferred_element_type=jnp.float32,
    )
    page_den = jnp.sum(weights, axis=-1) + jnp.sum(fresh_weights, axis=-1)
    head_count = QUERY_HEADS
    owner_cols = query_cols
    owner_heads = max(1, owner_cols // HEAD_WIDTH)
    head_repeat = min(owner_cols, HEAD_WIDTH)
    owner_first_head = [(o * owner_cols) // HEAD_WIDTH for o in range(device_count)]
    head_pick = jnp.asarray(
        [[first + j for j in range(owner_heads)] for first in owner_first_head], jnp.int32
    )
    slot_num = to_tokens(page_num).reshape(request_page_count, NEW_TOKENS, device_count, owner_cols)
    slot_den = to_tokens(page_den[..., None]).reshape(request_page_count, NEW_TOKENS, head_count)
    slot_peak = to_tokens(page_peak[..., None]).reshape(request_page_count, NEW_TOKENS, head_count)
    num_part, den_part, peak_part = [
        part.transpose(2, 0, 1, 3).reshape(device_count, request_page_count, -1)
        for part in (slot_num, slot_den[:, :, head_pick], slot_peak[:, :, head_pick])
    ]
    exact_part = jnp.concatenate([den_part, peak_part], axis=2)
    high = lax.reduce_precision(exact_part, exponent_bits=8, mantissa_bits=7)
    rest = exact_part - high
    middle = lax.reduce_precision(rest, exponent_bits=8, mantissa_bits=7)
    low = rest - middle
    packed = jnp.concatenate(
        [num_part.astype(jnp.bfloat16)] + [p.astype(jnp.bfloat16) for p in (high, middle, low)],
        axis=2,
    )
    arrived = lax.all_to_all(packed, "blk", 0, 0, tiled=True).reshape(group_pages, -1)
    num_width = NEW_TOKENS * owner_cols
    head_width = NEW_TOKENS * owner_heads
    arrived_num = arrived[:, :num_width].astype(jnp.float32)
    pieces = [
        arrived[:, num_width + k * 2 * head_width : num_width + (k + 1) * 2 * head_width].astype(
            jnp.float32
        )
        for k in range(3)
    ]
    arrived_exact = (pieces[0] + pieces[1]) + pieces[2]
    arrived_den = arrived_exact[:, :head_width]
    arrived_peak = arrived_exact[:, head_width:]
    top_flat = jnp.max(
        jnp.where(owner_of_page[:, None, :], arrived_peak.T[None], neg_large), axis=2
    )
    rescale = jnp.exp(arrived_peak - top_flat[page_of_req])
    rescaled = jnp.concatenate(
        [arrived_num * jnp.repeat(rescale, head_repeat, axis=1), arrived_den * rescale], axis=1
    )
    summed = jnp.einsum(
        "rp,px->rx", owner_of_page.astype(jnp.float32), rescaled, precision=lax.Precision.HIGHEST
    )
    num_own = summed[:, :num_width].reshape(request_count * NEW_TOKENS, owner_cols)
    den_own = summed[:, num_width:].reshape(request_count * NEW_TOKENS, owner_heads)
    attended_own = (num_own / jnp.repeat(den_own, head_repeat, axis=1)).astype(jnp.bfloat16)
    attended = lax.all_gather(attended_own, "blk", axis=1, tiled=True)
    return jnp.dot(attended, output_weight, preferred_element_type=jnp.float32).astype(jnp.bfloat16)


def solution(mesh):
    placed = (
        P("groups", "blk"),
        P(),
        P(None, "blk"),
        P(None, "blk"),
        P(None, "blk"),
        P("blk", None, None),
        P(None, None, "blk"),
        P(("groups", "blk"), None, None),
        P("groups"),
        P(),
        P("groups"),
        P("groups", None),
    )
    return jax.shard_map(
        local, mesh=mesh, in_specs=placed, out_specs=P("groups", "blk"), check_vma=False
    )
```

```python
import math

import jax
import jax.numpy as jnp
from jax import lax
from jax.experimental import pallas as pl
from jax.experimental.pallas import tpu as pltpu
from jax.sharding import PartitionSpec as P

QUERY_HEADS = 64
KEY_VALUE_HEADS = 8
HEAD_WIDTH = 128
PAGE_LENGTH = 128
NEW_TOKENS = 3


theta_base = 500000.0
neg_large = -1e30


def apply_rotation(values, token_positions, first_col, rot_limit):
    width_cols = values.shape[1]
    columns = first_col + jnp.arange(width_cols, dtype=jnp.int32)
    pair_index = (columns % HEAD_WIDTH // 2).astype(jnp.float32)
    inverse = jnp.exp(pair_index * (-2.0 * math.log(theta_base) / HEAD_WIDTH))
    angles = token_positions[:, None] * inverse[None, :]
    cos_val = jnp.cos(angles[:, 0::2])
    sine_val = jnp.sin(angles[:, 0::2])
    even_part = values[:, 0::2]
    odd_part = values[:, 1::2]
    turned = jnp.stack(
        [even_part * cos_val - odd_part * sine_val, even_part * sine_val + odd_part * cos_val],
        axis=-1,
    ).reshape(values.shape)
    return jnp.where((columns < rot_limit)[None, :], turned, values)


def rotation_kernel(base_ref, addend_ref, cos_ref, sine_ref, out_ref):
    values = base_ref[...] + addend_ref[...]
    width = values.shape[1]
    following = pltpu.roll(values, width - 1, 1)
    preceding = pltpu.roll(values, 1, 1)
    even = lax.broadcasted_iota(jnp.int32, values.shape, 1) % 2 == 0
    cos_val = cos_ref[...]
    sine_val = sine_ref[...]
    out_ref[...] = jnp.where(
        even, values * cos_val - following * sine_val, preceding * sine_val + values * cos_val
    ).astype(out_ref.dtype)


def rotate_columns(values, addend, token_positions, global_cols, rot_limit):
    pair_index = (global_cols % HEAD_WIDTH // 2).astype(jnp.float32)
    inverse = jnp.exp(pair_index * (-2.0 * math.log(theta_base) / HEAD_WIDTH))
    angles = token_positions[:, None] * inverse[None, :]
    rotated = (global_cols < rot_limit)[None, :]
    cos_val = jnp.where(rotated, jnp.cos(angles), 1.0)
    sine_val = jnp.where(rotated, jnp.sin(angles), 0.0)
    width = values.shape[1]
    pad = -(-width // 128) * 128 - width
    operands = [jnp.pad(a, ((0, 0), (0, pad))) for a in (values, addend, cos_val, sine_val)]
    out = pl.pallas_call(
        rotation_kernel,
        out_shape=jax.ShapeDtypeStruct(operands[0].shape, jnp.bfloat16),
    )(*operands)
    return out[:, :width]


def normalize(layer_input_tokens, input_norm_gain):
    values = layer_input_tokens.astype(jnp.float32)
    mean_square = jnp.mean(values * values, axis=-1, keepdims=True)
    return (values * lax.rsqrt(mean_square + 1e-05) * input_norm_gain[None, :]).astype(jnp.bfloat16)


def positions_of(cached_lengths):
    steps_row = jnp.arange(NEW_TOKENS, dtype=jnp.int32)
    return (
        jnp.repeat(cached_lengths, NEW_TOKENS) + jnp.tile(steps_row, cached_lengths.shape[0])
    ).astype(jnp.float32)


def to_tokens(request_first_layout):
    request_count = request_first_layout.shape[0]
    trailing_shape = request_first_layout.shape[3:]
    query_group_width = QUERY_HEADS // KEY_VALUE_HEADS
    split_head_shape = request_first_layout.reshape(
        (request_count, KEY_VALUE_HEADS, NEW_TOKENS, query_group_width) + trailing_shape
    )
    order_axes = (0, 2, 1, 3) + tuple(range(4, 4 + len(trailing_shape)))
    return split_head_shape.transpose(order_axes).reshape(request_count * NEW_TOKENS, -1)


def butterfly(value, combine):
    size = lax.axis_size("blk")
    step = 1
    while step < size:
        masks = [step] if step * 2 >= size else [step, step * 2, step * 3]
        arrived = [lax.ppermute(value, "blk", [(i, i ^ m) for i in range(size)]) for m in masks]
        for other in arrived:
            value = combine(value, other)
        step *= 2 ** len(masks[:2])
    return value


def local(
    layer_input_tokens,
    input_norm_gain,
    query_weight,
    key_value_weight,
    output_weight,
    adapter_down_weight,
    adapter_up_weight,
    key_value_page_pool,
    request_adapter,
    adapter_storage_slot,
    cached_lengths,
    request_page_tables,
):
    own_index = lax.axis_index("blk")
    gathered = lax.all_gather(layer_input_tokens, "blk", axis=1, tiled=True)
    normalized_input = normalize(gathered, input_norm_gain)
    request_count = cached_lengths.shape[0]
    adapter_total = adapter_storage_slot.shape[0]
    choose = request_adapter[:, None] == jnp.arange(adapter_total, dtype=jnp.int32)[None, :]
    req_slot = jnp.sum(jnp.where(choose, adapter_storage_slot[None, :], 0), axis=1)
    token_cache_slot = jnp.repeat(req_slot, NEW_TOKENS)
    local_token_count = adapter_down_weight.shape[0]
    local_pick = (
        token_cache_slot[:, None] - own_index * local_token_count
        == jnp.arange(local_token_count, dtype=jnp.int32)[None, :]
    )
    output_projected = jnp.einsum(
        "ly,mxy->lmx", normalized_input, adapter_down_weight, preferred_element_type=jnp.float32
    )
    partial_codes = jnp.sum(jnp.where(local_pick[:, :, None], output_projected, 0.0), axis=1)
    adapter_choice_index = butterfly(partial_codes.astype(jnp.bfloat16), jnp.add)
    slot_count, adapter_rank, _ = adapter_up_weight.shape
    slot_pick = token_cache_slot[:, None] == jnp.arange(slot_count, dtype=jnp.int32)[None, :]
    spread_codes = jnp.where(
        slot_pick[:, :, None], adapter_choice_index[:, None, :], jnp.zeros((), jnp.bfloat16)
    ).reshape(token_cache_slot.shape[0], slot_count * adapter_rank)
    adapter_query_update = jnp.dot(
        spread_codes,
        adapter_up_weight.reshape(slot_count * adapter_rank, -1),
        preferred_element_type=jnp.float32,
    )
    token_positions = positions_of(cached_lengths)
    query_cols = query_weight.shape[1]
    keyval_cols = key_value_weight.shape[1]
    both_parts = jnp.concatenate(
        [
            jnp.dot(normalized_input, query_weight, preferred_element_type=jnp.float32),
            jnp.dot(normalized_input, key_value_weight, preferred_element_type=jnp.float32),
        ],
        axis=1,
    )
    both_addends = jnp.concatenate(
        [
            adapter_query_update,
            jnp.zeros((adapter_query_update.shape[0], keyval_cols), jnp.float32),
        ],
        axis=1,
    )
    global_cols = jnp.concatenate(
        [
            own_index * query_cols + jnp.arange(query_cols, dtype=jnp.int32),
            own_index * keyval_cols + jnp.arange(keyval_cols, dtype=jnp.int32),
        ]
    )
    limits = jnp.concatenate(
        [
            jnp.full((query_cols,), QUERY_HEADS * HEAD_WIDTH, jnp.int32),
            jnp.full((keyval_cols,), KEY_VALUE_HEADS * HEAD_WIDTH, jnp.int32),
        ]
    )
    rotated_parts = rotate_columns(both_parts, both_addends, token_positions, global_cols, limits)
    device_count = lax.axis_size("blk")
    request_page_count = key_value_page_pool.shape[0]
    table_width = request_page_tables.shape[1]
    group_pages = device_count * request_page_count
    listed_pages = request_page_tables.reshape(-1)
    listed_target = jnp.where(listed_pages >= 0, listed_pages, group_pages)
    page_of_req = (
        jnp.zeros((group_pages,), jnp.int32)
        .at[listed_target]
        .set(jnp.repeat(jnp.arange(request_count, dtype=jnp.int32), table_width), mode="drop")
    )
    page_used = jnp.zeros((group_pages,), jnp.bool_).at[listed_target].set(True, mode="drop")
    owner_of_page = (
        jnp.arange(request_count, dtype=jnp.int32)[:, None] == page_of_req[None, :]
    ) & page_used[None, :]
    part_rows = rotated_parts.reshape(request_count, NEW_TOKENS, -1)
    part_width = part_rows.shape[2]
    outgoing = part_rows[page_of_req].reshape(
        device_count, request_page_count, NEW_TOKENS * part_width
    )
    incoming = (
        lax.all_to_all(outgoing, "blk", 0, 0, tiled=True)
        .reshape(device_count, request_page_count, NEW_TOKENS, part_width)
        .transpose(1, 2, 0, 3)
    )
    slot_queries = incoming[..., :query_cols].reshape(request_page_count, NEW_TOKENS, -1)
    slot_fresh = incoming[..., query_cols:].reshape(
        request_page_count, NEW_TOKENS, 2, KEY_VALUE_HEADS, HEAD_WIDTH
    )
    query_group_width = QUERY_HEADS // KEY_VALUE_HEADS
    query_feature_width = query_group_width * NEW_TOKENS
    score_scale = 1.0 / math.sqrt(HEAD_WIDTH)
    page_ids = own_index * request_page_count + jnp.arange(request_page_count, dtype=jnp.int32)
    matches = request_page_tables[None, :, :] == page_ids[:, None, None]
    page_owner = jnp.any(matches, axis=2)
    page_live = jnp.any(page_owner, axis=1)
    page_slot = jnp.sum(
        jnp.where(matches, jnp.arange(table_width, dtype=jnp.int32)[None, None, :], 0), axis=(1, 2)
    )
    page_len = jnp.sum(jnp.where(page_owner, cached_lengths[None, :], 0), axis=1)
    key_pos = page_slot[:, None] * PAGE_LENGTH + jnp.arange(PAGE_LENGTH, dtype=jnp.int32)[None, :]
    key_valid = page_live[:, None] & (key_pos < page_len[:, None])
    valid_full = key_valid[:, None, None, :]
    takes_fresh = page_live & (page_slot == 0)
    step_of = jnp.arange(query_feature_width, dtype=jnp.int32) // query_group_width
    fresh_valid = takes_fresh[:, None, None, None] & (
        jnp.arange(NEW_TOKENS, dtype=jnp.int32)[None, None, None, :] <= step_of[None, None, :, None]
    )
    cache_pages = key_value_page_pool.reshape(
        request_page_count, PAGE_LENGTH, 2, KEY_VALUE_HEADS, HEAD_WIDTH
    )
    query_page = (
        slot_queries.reshape(
            request_page_count, NEW_TOKENS, KEY_VALUE_HEADS, query_group_width, HEAD_WIDTH
        )
        .transpose(0, 2, 1, 3, 4)
        .reshape(request_page_count, KEY_VALUE_HEADS, query_feature_width, HEAD_WIDTH)
    )
    scores = (
        jnp.einsum(
            "skqd,spkd->skqp", query_page, cache_pages[:, :, 0], preferred_element_type=jnp.float32
        )
        * score_scale
    )
    fresh_scores = (
        jnp.einsum(
            "skqd,sjkd->skqj", query_page, slot_fresh[:, :, 0], preferred_element_type=jnp.float32
        )
        * score_scale
    )
    masked = jnp.where(valid_full, scores, neg_large)
    fresh_masked = jnp.where(fresh_valid, fresh_scores, neg_large)
    page_peak = jnp.maximum(jnp.max(masked, axis=-1), jnp.max(fresh_masked, axis=-1))
    weights = jnp.where(valid_full, jnp.exp(masked - page_peak[..., None]), 0.0)
    fresh_weights = jnp.where(fresh_valid, jnp.exp(fresh_masked - page_peak[..., None]), 0.0)
    page_num = jnp.einsum(
        "skqp,spkd->skqd",
        weights.astype(jnp.bfloat16),
        cache_pages[:, :, 1],
        preferred_element_type=jnp.float32,
    ) + jnp.einsum(
        "skqj,sjkd->skqd",
        fresh_weights.astype(jnp.bfloat16),
        slot_fresh[:, :, 1],
        preferred_element_type=jnp.float32,
    )
    page_den = jnp.sum(weights, axis=-1) + jnp.sum(fresh_weights, axis=-1)
    head_count = QUERY_HEADS
    owner_cols = query_cols
    owner_heads = max(1, owner_cols // HEAD_WIDTH)
    head_repeat = min(owner_cols, HEAD_WIDTH)
    owner_first_head = [(o * owner_cols) // HEAD_WIDTH for o in range(device_count)]
    head_pick = jnp.asarray(
        [[first + j for j in range(owner_heads)] for first in owner_first_head], jnp.int32
    )
    slot_num = to_tokens(page_num).reshape(request_page_count, NEW_TOKENS, device_count, owner_cols)
    slot_den = to_tokens(page_den[..., None]).reshape(request_page_count, NEW_TOKENS, head_count)
    slot_peak = to_tokens(page_peak[..., None]).reshape(request_page_count, NEW_TOKENS, head_count)
    packed = jnp.concatenate(
        [
            part.transpose(2, 0, 1, 3).reshape(device_count, request_page_count, -1)
            for part in (slot_num, slot_den[:, :, head_pick], slot_peak[:, :, head_pick])
        ],
        axis=2,
    )
    arrived = lax.all_to_all(packed, "blk", 0, 0, tiled=True).reshape(group_pages, -1)
    num_width = NEW_TOKENS * owner_cols
    head_width = NEW_TOKENS * owner_heads
    arrived_num = arrived[:, :num_width]
    arrived_den = arrived[:, num_width : num_width + head_width]
    arrived_peak = arrived[:, num_width + head_width :]
    top_flat = jnp.max(
        jnp.where(owner_of_page[:, None, :], arrived_peak.T[None], neg_large), axis=2
    )
    rescale = jnp.exp(arrived_peak - top_flat[page_of_req])
    rescaled = jnp.concatenate(
        [arrived_num * jnp.repeat(rescale, head_repeat, axis=1), arrived_den * rescale], axis=1
    )
    summed = jnp.einsum(
        "rp,px->rx", owner_of_page.astype(jnp.float32), rescaled, precision=lax.Precision.HIGHEST
    )
    num_own = summed[:, :num_width].reshape(request_count * NEW_TOKENS, owner_cols)
    den_own = summed[:, num_width:].reshape(request_count * NEW_TOKENS, owner_heads)
    attended_own = (num_own / jnp.repeat(den_own, head_repeat, axis=1)).astype(jnp.bfloat16)
    attended = lax.all_gather(attended_own, "blk", axis=1, tiled=True)
    return jnp.dot(attended, output_weight, preferred_element_type=jnp.float32).astype(jnp.bfloat16)


def solution(mesh):
    placed = (
        P("groups", "blk"),
        P(),
        P(None, "blk"),
        P(None, "blk"),
        P(None, "blk"),
        P("blk", None, None),
        P(None, None, "blk"),
        P(("groups", "blk"), None, None),
        P("groups"),
        P(),
        P("groups"),
        P("groups", None),
    )
    return jax.shard_map(
        local, mesh=mesh, in_specs=placed, out_specs=P("groups", "blk"), check_vma=False
    )
```

```python
import math

import jax
import jax.numpy as jnp
from jax import lax
from jax.experimental import pallas as pl
from jax.experimental.pallas import tpu as pltpu
from jax.sharding import PartitionSpec as P

QUERY_HEADS = 64
KEY_VALUE_HEADS = 8
HEAD_WIDTH = 128
PAGE_LENGTH = 128
NEW_TOKENS = 3


theta_base = 500000.0
neg_large = -1e30


def apply_rotation(values, token_positions, first_col, rot_limit):
    width_cols = values.shape[1]
    columns = first_col + jnp.arange(width_cols, dtype=jnp.int32)
    pair_index = (columns % HEAD_WIDTH // 2).astype(jnp.float32)
    inverse = jnp.exp(pair_index * (-2.0 * math.log(theta_base) / HEAD_WIDTH))
    angles = token_positions[:, None] * inverse[None, :]
    cos_val = jnp.cos(angles[:, 0::2])
    sine_val = jnp.sin(angles[:, 0::2])
    even_part = values[:, 0::2]
    odd_part = values[:, 1::2]
    turned = jnp.stack(
        [even_part * cos_val - odd_part * sine_val, even_part * sine_val + odd_part * cos_val],
        axis=-1,
    ).reshape(values.shape)
    return jnp.where((columns < rot_limit)[None, :], turned, values)


def rotation_kernel(base_ref, addend_ref, cos_ref, sine_ref, out_ref):
    values = base_ref[...] + addend_ref[...]
    width = values.shape[1]
    following = pltpu.roll(values, width - 1, 1)
    preceding = pltpu.roll(values, 1, 1)
    even = lax.broadcasted_iota(jnp.int32, values.shape, 1) % 2 == 0
    cos_val = cos_ref[...]
    sine_val = sine_ref[...]
    out_ref[...] = jnp.where(
        even, values * cos_val - following * sine_val, preceding * sine_val + values * cos_val
    ).astype(out_ref.dtype)


def rotate_columns(values, addend, token_positions, global_cols, rot_limit):
    pair_index = (global_cols % HEAD_WIDTH // 2).astype(jnp.float32)
    inverse = jnp.exp(pair_index * (-2.0 * math.log(theta_base) / HEAD_WIDTH))
    angles = token_positions[:, None] * inverse[None, :]
    rotated = (global_cols < rot_limit)[None, :]
    cos_val = jnp.where(rotated, jnp.cos(angles), 1.0)
    sine_val = jnp.where(rotated, jnp.sin(angles), 0.0)
    width = values.shape[1]
    pad = -(-width // 128) * 128 - width
    operands = [jnp.pad(a, ((0, 0), (0, pad))) for a in (values, addend, cos_val, sine_val)]
    out = pl.pallas_call(
        rotation_kernel,
        out_shape=jax.ShapeDtypeStruct(operands[0].shape, jnp.bfloat16),
    )(*operands)
    return out[:, :width]


def normalize(layer_input_tokens, input_norm_gain):
    values = layer_input_tokens.astype(jnp.float32)
    mean_square = jnp.mean(values * values, axis=-1, keepdims=True)
    return (values * lax.rsqrt(mean_square + 1e-05) * input_norm_gain[None, :]).astype(jnp.bfloat16)


def positions_of(cached_lengths):
    steps_row = jnp.arange(NEW_TOKENS, dtype=jnp.int32)
    return (
        jnp.repeat(cached_lengths, NEW_TOKENS) + jnp.tile(steps_row, cached_lengths.shape[0])
    ).astype(jnp.float32)


def to_tokens(request_first_layout):
    request_count = request_first_layout.shape[0]
    trailing_shape = request_first_layout.shape[3:]
    query_group_width = QUERY_HEADS // KEY_VALUE_HEADS
    split_head_shape = request_first_layout.reshape(
        (request_count, KEY_VALUE_HEADS, NEW_TOKENS, query_group_width) + trailing_shape
    )
    order_axes = (0, 2, 1, 3) + tuple(range(4, 4 + len(trailing_shape)))
    return split_head_shape.transpose(order_axes).reshape(request_count * NEW_TOKENS, -1)


def butterfly(value, combine):
    size = lax.axis_size("blk")
    step = 1
    while step < size:
        masks = [step] if step * 2 >= size else [step, step * 2, step * 3]
        arrived = [lax.ppermute(value, "blk", [(i, i ^ m) for i in range(size)]) for m in masks]
        for other in arrived:
            value = combine(value, other)
        step *= 2 ** len(masks[:2])
    return value


def local(
    layer_input_tokens,
    input_norm_gain,
    query_weight,
    key_value_weight,
    output_weight,
    adapter_down_weight,
    adapter_up_weight,
    key_value_page_pool,
    request_adapter,
    adapter_storage_slot,
    cached_lengths,
    request_page_tables,
):
    own_index = lax.axis_index("blk")
    gathered = lax.all_gather(layer_input_tokens, "blk", axis=1, tiled=True)
    normalized_input = normalize(gathered, input_norm_gain)
    request_count = cached_lengths.shape[0]
    adapter_total = adapter_storage_slot.shape[0]
    choose = request_adapter[:, None] == jnp.arange(adapter_total, dtype=jnp.int32)[None, :]
    req_slot = jnp.sum(jnp.where(choose, adapter_storage_slot[None, :], 0), axis=1)
    token_cache_slot = jnp.repeat(req_slot, NEW_TOKENS)
    local_token_count = adapter_down_weight.shape[0]
    local_pick = (
        token_cache_slot[:, None] - own_index * local_token_count
        == jnp.arange(local_token_count, dtype=jnp.int32)[None, :]
    )
    output_projected = jnp.einsum(
        "ly,mxy->lmx", normalized_input, adapter_down_weight, preferred_element_type=jnp.float32
    )
    partial_codes = jnp.sum(jnp.where(local_pick[:, :, None], output_projected, 0.0), axis=1)
    adapter_choice_index = butterfly(partial_codes.astype(jnp.bfloat16), jnp.add)
    slot_count, adapter_rank, _ = adapter_up_weight.shape
    slot_pick = token_cache_slot[:, None] == jnp.arange(slot_count, dtype=jnp.int32)[None, :]
    spread_codes = jnp.where(
        slot_pick[:, :, None], adapter_choice_index[:, None, :], jnp.zeros((), jnp.bfloat16)
    ).reshape(token_cache_slot.shape[0], slot_count * adapter_rank)
    adapter_query_update = jnp.dot(
        spread_codes,
        adapter_up_weight.reshape(slot_count * adapter_rank, -1),
        preferred_element_type=jnp.float32,
    )
    token_positions = positions_of(cached_lengths)
    query_cols = query_weight.shape[1]
    keyval_cols = key_value_weight.shape[1]
    both_parts = jnp.concatenate(
        [
            jnp.dot(normalized_input, query_weight, preferred_element_type=jnp.float32),
            jnp.dot(normalized_input, key_value_weight, preferred_element_type=jnp.float32),
        ],
        axis=1,
    )
    both_addends = jnp.concatenate(
        [
            adapter_query_update,
            jnp.zeros((adapter_query_update.shape[0], keyval_cols), jnp.float32),
        ],
        axis=1,
    )
    global_cols = jnp.concatenate(
        [
            own_index * query_cols + jnp.arange(query_cols, dtype=jnp.int32),
            own_index * keyval_cols + jnp.arange(keyval_cols, dtype=jnp.int32),
        ]
    )
    limits = jnp.concatenate(
        [
            jnp.full((query_cols,), QUERY_HEADS * HEAD_WIDTH, jnp.int32),
            jnp.full((keyval_cols,), KEY_VALUE_HEADS * HEAD_WIDTH, jnp.int32),
        ]
    )
    rotated_parts = rotate_columns(both_parts, both_addends, token_positions, global_cols, limits)
    device_count = lax.axis_size("blk")
    request_page_count = key_value_page_pool.shape[0]
    table_width = request_page_tables.shape[1]
    group_pages = device_count * request_page_count
    listed_pages = request_page_tables.reshape(-1)
    listed_target = jnp.where(listed_pages >= 0, listed_pages, group_pages)
    page_of_req = (
        jnp.zeros((group_pages,), jnp.int32)
        .at[listed_target]
        .set(jnp.repeat(jnp.arange(request_count, dtype=jnp.int32), table_width), mode="drop")
    )
    page_used = jnp.zeros((group_pages,), jnp.bool_).at[listed_target].set(True, mode="drop")
    owner_of_page = (
        jnp.arange(request_count, dtype=jnp.int32)[:, None] == page_of_req[None, :]
    ) & page_used[None, :]
    part_rows = rotated_parts.reshape(request_count, NEW_TOKENS, -1)
    part_width = part_rows.shape[2]
    outgoing = part_rows[page_of_req].reshape(
        device_count, request_page_count, NEW_TOKENS * part_width
    )
    incoming = (
        lax.all_to_all(outgoing, "blk", 0, 0, tiled=True)
        .reshape(device_count, request_page_count, NEW_TOKENS, part_width)
        .transpose(1, 2, 0, 3)
    )
    slot_queries = incoming[..., :query_cols].reshape(request_page_count, NEW_TOKENS, -1)
    slot_fresh = incoming[..., query_cols:].reshape(
        request_page_count, NEW_TOKENS, 2, KEY_VALUE_HEADS, HEAD_WIDTH
    )
    query_group_width = QUERY_HEADS // KEY_VALUE_HEADS
    query_feature_width = query_group_width * NEW_TOKENS
    score_scale = 1.0 / math.sqrt(HEAD_WIDTH)
    page_ids = own_index * request_page_count + jnp.arange(request_page_count, dtype=jnp.int32)
    matches = request_page_tables[None, :, :] == page_ids[:, None, None]
    page_owner = jnp.any(matches, axis=2)
    page_live = jnp.any(page_owner, axis=1)
    page_slot = jnp.sum(
        jnp.where(matches, jnp.arange(table_width, dtype=jnp.int32)[None, None, :], 0), axis=(1, 2)
    )
    page_len = jnp.sum(jnp.where(page_owner, cached_lengths[None, :], 0), axis=1)
    key_pos = page_slot[:, None] * PAGE_LENGTH + jnp.arange(PAGE_LENGTH, dtype=jnp.int32)[None, :]
    key_valid = page_live[:, None] & (key_pos < page_len[:, None])
    valid_full = key_valid[:, None, None, :]
    takes_fresh = page_live & (page_slot == 0)
    step_of = jnp.arange(query_feature_width, dtype=jnp.int32) // query_group_width
    fresh_valid = takes_fresh[:, None, None, None] & (
        jnp.arange(NEW_TOKENS, dtype=jnp.int32)[None, None, None, :] <= step_of[None, None, :, None]
    )
    cache_pages = key_value_page_pool.reshape(
        request_page_count, PAGE_LENGTH, 2, KEY_VALUE_HEADS, HEAD_WIDTH
    )
    query_page = (
        slot_queries.reshape(
            request_page_count, NEW_TOKENS, KEY_VALUE_HEADS, query_group_width, HEAD_WIDTH
        )
        .transpose(0, 2, 1, 3, 4)
        .reshape(request_page_count, KEY_VALUE_HEADS, query_feature_width, HEAD_WIDTH)
    )
    scores = (
        jnp.einsum(
            "skqd,spkd->skqp", query_page, cache_pages[:, :, 0], preferred_element_type=jnp.float32
        )
        * score_scale
    )
    fresh_scores = (
        jnp.einsum(
            "skqd,sjkd->skqj", query_page, slot_fresh[:, :, 0], preferred_element_type=jnp.float32
        )
        * score_scale
    )
    masked = jnp.where(valid_full, scores, neg_large)
    fresh_masked = jnp.where(fresh_valid, fresh_scores, neg_large)
    page_peak = jnp.maximum(jnp.max(masked, axis=-1), jnp.max(fresh_masked, axis=-1))
    weights = jnp.where(valid_full, jnp.exp(masked - page_peak[..., None]), 0.0)
    fresh_weights = jnp.where(fresh_valid, jnp.exp(fresh_masked - page_peak[..., None]), 0.0)
    page_num = jnp.einsum(
        "skqp,spkd->ksqd",
        weights.astype(jnp.bfloat16),
        cache_pages[:, :, 1],
        preferred_element_type=jnp.float32,
    ) + jnp.einsum(
        "skqj,sjkd->ksqd",
        fresh_weights.astype(jnp.bfloat16),
        slot_fresh[:, :, 1],
        preferred_element_type=jnp.float32,
    )
    page_den = jnp.sum(weights, axis=-1) + jnp.sum(fresh_weights, axis=-1)
    head_count = QUERY_HEADS
    owner_cols = query_cols
    owner_heads = max(1, owner_cols // HEAD_WIDTH)
    head_repeat = min(owner_cols, HEAD_WIDTH)
    owner_first_head = [(o * owner_cols) // HEAD_WIDTH for o in range(device_count)]
    head_pick = jnp.asarray(
        [[first + j for j in range(owner_heads)] for first in owner_first_head], jnp.int32
    )
    owners_per_group = (query_group_width * HEAD_WIDTH) // owner_cols
    num_part = (
        page_num.reshape(
            KEY_VALUE_HEADS, request_page_count, NEW_TOKENS, owners_per_group, owner_cols
        )
        .transpose(0, 3, 1, 2, 4)
        .reshape(device_count, request_page_count, NEW_TOKENS * owner_cols)
    )
    slot_den = to_tokens(page_den[..., None]).reshape(request_page_count, NEW_TOKENS, head_count)
    slot_peak = to_tokens(page_peak[..., None]).reshape(request_page_count, NEW_TOKENS, head_count)
    packed = jnp.concatenate(
        [num_part]
        + [
            part.transpose(2, 0, 1, 3).reshape(device_count, request_page_count, -1)
            for part in (slot_den[:, :, head_pick], slot_peak[:, :, head_pick])
        ],
        axis=2,
    )
    arrived = lax.all_to_all(packed, "blk", 0, 0, tiled=True).reshape(group_pages, -1)
    num_width = NEW_TOKENS * owner_cols
    head_width = NEW_TOKENS * owner_heads
    arrived_num = arrived[:, :num_width]
    arrived_den = arrived[:, num_width : num_width + head_width]
    arrived_peak = arrived[:, num_width + head_width :]
    top_flat = jnp.max(
        jnp.where(owner_of_page[:, None, :], arrived_peak.T[None], neg_large), axis=2
    )
    rescale = jnp.exp(arrived_peak - top_flat[page_of_req])
    rescaled = jnp.concatenate(
        [arrived_num * jnp.repeat(rescale, head_repeat, axis=1), arrived_den * rescale], axis=1
    )
    summed = jnp.einsum(
        "rp,px->rx", owner_of_page.astype(jnp.float32), rescaled, precision=lax.Precision.HIGHEST
    )
    num_own = summed[:, :num_width].reshape(request_count * NEW_TOKENS, owner_cols)
    den_own = summed[:, num_width:].reshape(request_count * NEW_TOKENS, owner_heads)
    attended_own = (num_own / jnp.repeat(den_own, head_repeat, axis=1)).astype(jnp.bfloat16)
    attended = lax.all_gather(attended_own, "blk", axis=1, tiled=True)
    return jnp.dot(attended, output_weight, preferred_element_type=jnp.float32).astype(jnp.bfloat16)


def solution(mesh):
    placed = (
        P("groups", "blk"),
        P(),
        P(None, "blk"),
        P(None, "blk"),
        P(None, "blk"),
        P("blk", None, None),
        P(None, None, "blk"),
        P(("groups", "blk"), None, None),
        P("groups"),
        P(),
        P("groups"),
        P("groups", None),
    )
    return jax.shard_map(
        local, mesh=mesh, in_specs=placed, out_specs=P("groups", "blk"), check_vma=False
    )
```

```python
import math

import jax
import jax.numpy as jnp
from jax import lax
from jax.experimental import pallas as pl
from jax.experimental.pallas import tpu as pltpu
from jax.sharding import PartitionSpec as P

QUERY_HEADS = 64
KEY_VALUE_HEADS = 8
HEAD_WIDTH = 128
PAGE_LENGTH = 128
NEW_TOKENS = 3


theta_base = 500000.0
neg_large = -1e30


def apply_rotation(values, token_positions, first_col, rot_limit):
    width_cols = values.shape[1]
    columns = first_col + jnp.arange(width_cols, dtype=jnp.int32)
    pair_index = (columns % HEAD_WIDTH // 2).astype(jnp.float32)
    inverse = jnp.exp(pair_index * (-2.0 * math.log(theta_base) / HEAD_WIDTH))
    angles = token_positions[:, None] * inverse[None, :]
    cos_val = jnp.cos(angles[:, 0::2])
    sine_val = jnp.sin(angles[:, 0::2])
    even_part = values[:, 0::2]
    odd_part = values[:, 1::2]
    turned = jnp.stack(
        [even_part * cos_val - odd_part * sine_val, even_part * sine_val + odd_part * cos_val],
        axis=-1,
    ).reshape(values.shape)
    return jnp.where((columns < rot_limit)[None, :], turned, values)


def rotation_kernel(values_ref, cos_ref, sine_ref, out_ref):
    values = values_ref[...]
    width = values.shape[1]
    following = pltpu.roll(values, width - 1, 1)
    preceding = pltpu.roll(values, 1, 1)
    even = lax.broadcasted_iota(jnp.int32, values.shape, 1) % 2 == 0
    cos_val = cos_ref[...]
    sine_val = sine_ref[...]
    out_ref[...] = jnp.where(
        even, values * cos_val - following * sine_val, preceding * sine_val + values * cos_val
    ).astype(out_ref.dtype)


def rotate_columns(values, token_positions, global_cols, rot_limit):
    pair_index = (global_cols % HEAD_WIDTH // 2).astype(jnp.float32)
    inverse = jnp.exp(pair_index * (-2.0 * math.log(theta_base) / HEAD_WIDTH))
    angles = token_positions[:, None] * inverse[None, :]
    rotated = (global_cols < rot_limit)[None, :]
    cos_val = jnp.where(rotated, jnp.cos(angles), 1.0)
    sine_val = jnp.where(rotated, jnp.sin(angles), 0.0)
    width = values.shape[1]
    pad = -(-width // 128) * 128 - width
    operands = [jnp.pad(a, ((0, 0), (0, pad))) for a in (values, cos_val, sine_val)]
    out = pl.pallas_call(
        rotation_kernel,
        out_shape=jax.ShapeDtypeStruct(operands[0].shape, jnp.bfloat16),
    )(*operands)
    return out[:, :width]


def normalize(layer_input_tokens, input_norm_gain):
    values = layer_input_tokens.astype(jnp.float32)
    mean_square = jnp.mean(values * values, axis=-1, keepdims=True)
    return (values * lax.rsqrt(mean_square + 1e-05) * input_norm_gain[None, :]).astype(jnp.bfloat16)


def positions_of(cached_lengths):
    steps_row = jnp.arange(NEW_TOKENS, dtype=jnp.int32)
    return (
        jnp.repeat(cached_lengths, NEW_TOKENS) + jnp.tile(steps_row, cached_lengths.shape[0])
    ).astype(jnp.float32)


def to_tokens(request_first_layout):
    request_count = request_first_layout.shape[0]
    trailing_shape = request_first_layout.shape[3:]
    query_group_width = QUERY_HEADS // KEY_VALUE_HEADS
    split_head_shape = request_first_layout.reshape(
        (request_count, KEY_VALUE_HEADS, NEW_TOKENS, query_group_width) + trailing_shape
    )
    order_axes = (0, 2, 1, 3) + tuple(range(4, 4 + len(trailing_shape)))
    return split_head_shape.transpose(order_axes).reshape(request_count * NEW_TOKENS, -1)


def butterfly(value, combine):
    size = lax.axis_size("blk")
    step = 1
    while step < size:
        masks = [step] if step * 2 >= size else [step, step * 2, step * 3]
        arrived = [lax.ppermute(value, "blk", [(i, i ^ m) for i in range(size)]) for m in masks]
        for other in arrived:
            value = combine(value, other)
        step *= 2 ** len(masks[:2])
    return value


def local(
    layer_input_tokens,
    input_norm_gain,
    query_weight,
    key_value_weight,
    output_weight,
    adapter_down_weight,
    adapter_up_weight,
    key_value_page_pool,
    request_adapter,
    adapter_storage_slot,
    cached_lengths,
    request_page_tables,
):
    own_index = lax.axis_index("blk")
    gathered = lax.all_gather(layer_input_tokens, "blk", axis=1, tiled=True)
    normalized_input = normalize(gathered, input_norm_gain)
    request_count = cached_lengths.shape[0]
    adapter_total = adapter_storage_slot.shape[0]
    choose = request_adapter[:, None] == jnp.arange(adapter_total, dtype=jnp.int32)[None, :]
    req_slot = jnp.sum(jnp.where(choose, adapter_storage_slot[None, :], 0), axis=1)
    token_cache_slot = jnp.repeat(req_slot, NEW_TOKENS)
    local_token_count = adapter_down_weight.shape[0]
    local_pick = (
        token_cache_slot[:, None] - own_index * local_token_count
        == jnp.arange(local_token_count, dtype=jnp.int32)[None, :]
    )
    output_projected = jnp.einsum(
        "ly,mxy->lmx", normalized_input, adapter_down_weight, preferred_element_type=jnp.float32
    )
    partial_codes = jnp.sum(jnp.where(local_pick[:, :, None], output_projected, 0.0), axis=1)
    adapter_choice_index = butterfly(partial_codes.astype(jnp.bfloat16), jnp.add)
    slot_count, adapter_rank, _ = adapter_up_weight.shape
    slot_pick = token_cache_slot[:, None] == jnp.arange(slot_count, dtype=jnp.int32)[None, :]
    spread_codes = jnp.where(
        slot_pick[:, :, None], adapter_choice_index[:, None, :], jnp.zeros((), jnp.bfloat16)
    ).reshape(token_cache_slot.shape[0], slot_count * adapter_rank)
    adapter_query_update = jnp.dot(
        spread_codes,
        adapter_up_weight.reshape(slot_count * adapter_rank, -1),
        preferred_element_type=jnp.float32,
    )
    token_positions = positions_of(cached_lengths)
    query_cols = query_weight.shape[1]
    keyval_cols = key_value_weight.shape[1]
    both_parts = jnp.concatenate(
        [
            jnp.dot(normalized_input, query_weight, preferred_element_type=jnp.float32)
            + adapter_query_update,
            jnp.dot(normalized_input, key_value_weight, preferred_element_type=jnp.float32),
        ],
        axis=1,
    )
    global_cols = jnp.concatenate(
        [
            own_index * query_cols + jnp.arange(query_cols, dtype=jnp.int32),
            own_index * keyval_cols + jnp.arange(keyval_cols, dtype=jnp.int32),
        ]
    )
    limits = jnp.concatenate(
        [
            jnp.full((query_cols,), QUERY_HEADS * HEAD_WIDTH, jnp.int32),
            jnp.full((keyval_cols,), KEY_VALUE_HEADS * HEAD_WIDTH, jnp.int32),
        ]
    )
    rotated_parts = rotate_columns(both_parts, token_positions, global_cols, limits)
    device_count = lax.axis_size("blk")
    request_page_count = key_value_page_pool.shape[0]
    table_width = request_page_tables.shape[1]
    group_pages = device_count * request_page_count
    listed_pages = request_page_tables.reshape(-1)
    listed_target = jnp.where(listed_pages >= 0, listed_pages, group_pages)
    page_of_req = (
        jnp.zeros((group_pages,), jnp.int32)
        .at[listed_target]
        .set(jnp.repeat(jnp.arange(request_count, dtype=jnp.int32), table_width), mode="drop")
    )
    page_used = jnp.zeros((group_pages,), jnp.bool_).at[listed_target].set(True, mode="drop")
    owner_of_page = (
        jnp.arange(request_count, dtype=jnp.int32)[:, None] == page_of_req[None, :]
    ) & page_used[None, :]
    part_rows = rotated_parts.reshape(request_count, NEW_TOKENS, -1)
    part_width = part_rows.shape[2]
    outgoing = part_rows[page_of_req].reshape(
        device_count, request_page_count, NEW_TOKENS * part_width
    )
    incoming = (
        lax.all_to_all(outgoing, "blk", 0, 0, tiled=True)
        .reshape(device_count, request_page_count, NEW_TOKENS, part_width)
        .transpose(1, 2, 0, 3)
    )
    slot_queries = incoming[..., :query_cols].reshape(request_page_count, NEW_TOKENS, -1)
    slot_fresh = incoming[..., query_cols:].reshape(
        request_page_count, NEW_TOKENS, 2, KEY_VALUE_HEADS, HEAD_WIDTH
    )
    query_group_width = QUERY_HEADS // KEY_VALUE_HEADS
    query_feature_width = query_group_width * NEW_TOKENS
    score_scale = 1.0 / math.sqrt(HEAD_WIDTH)
    page_ids = own_index * request_page_count + jnp.arange(request_page_count, dtype=jnp.int32)
    matches = request_page_tables[None, :, :] == page_ids[:, None, None]
    page_owner = jnp.any(matches, axis=2)
    page_live = jnp.any(page_owner, axis=1)
    page_slot = jnp.sum(
        jnp.where(matches, jnp.arange(table_width, dtype=jnp.int32)[None, None, :], 0), axis=(1, 2)
    )
    page_len = jnp.sum(jnp.where(page_owner, cached_lengths[None, :], 0), axis=1)
    key_pos = page_slot[:, None] * PAGE_LENGTH + jnp.arange(PAGE_LENGTH, dtype=jnp.int32)[None, :]
    key_valid = page_live[:, None] & (key_pos < page_len[:, None])
    valid_full = key_valid[:, None, None, :]
    takes_fresh = page_live & (page_slot == 0)
    step_of = jnp.arange(query_feature_width, dtype=jnp.int32) // query_group_width
    fresh_valid = takes_fresh[:, None, None, None] & (
        jnp.arange(NEW_TOKENS, dtype=jnp.int32)[None, None, None, :] <= step_of[None, None, :, None]
    )
    cache_pages = key_value_page_pool.reshape(
        request_page_count, PAGE_LENGTH, 2, KEY_VALUE_HEADS, HEAD_WIDTH
    )
    head_count = QUERY_HEADS
    owner_cols = query_cols
    owner_heads = max(1, owner_cols // HEAD_WIDTH)
    head_repeat = min(owner_cols, HEAD_WIDTH)
    owner_first_head = [(o * owner_cols) // HEAD_WIDTH for o in range(device_count)]
    head_pick = jnp.asarray(
        [[first + j for j in range(owner_heads)] for first in owner_first_head], jnp.int32
    )

    def page_exchange(first, chunk_pages):
        chunk_queries = slot_queries[first : first + chunk_pages]
        chunk_cache = cache_pages[first : first + chunk_pages]
        chunk_fresh = slot_fresh[first : first + chunk_pages]
        chunk_valid = valid_full[first : first + chunk_pages]
        chunk_fresh_valid = fresh_valid[first : first + chunk_pages]
        query_page = (
            chunk_queries.reshape(
                chunk_pages, NEW_TOKENS, KEY_VALUE_HEADS, query_group_width, HEAD_WIDTH
            )
            .transpose(0, 2, 1, 3, 4)
            .reshape(chunk_pages, KEY_VALUE_HEADS, query_feature_width, HEAD_WIDTH)
        )
        scores = (
            jnp.einsum(
                "skqd,spkd->skqp", query_page, chunk_cache[:, :, 0], preferred_element_type=jnp.float32
            )
            * score_scale
        )
        fresh_scores = (
            jnp.einsum(
                "skqd,sjkd->skqj", query_page, chunk_fresh[:, :, 0], preferred_element_type=jnp.float32
            )
            * score_scale
        )
        masked = jnp.where(chunk_valid, scores, neg_large)
        fresh_masked = jnp.where(chunk_fresh_valid, fresh_scores, neg_large)
        page_peak = jnp.maximum(jnp.max(masked, axis=-1), jnp.max(fresh_masked, axis=-1))
        weights = jnp.where(chunk_valid, jnp.exp(masked - page_peak[..., None]), 0.0)
        fresh_weights = jnp.where(chunk_fresh_valid, jnp.exp(fresh_masked - page_peak[..., None]), 0.0)
        page_num = jnp.einsum(
            "skqp,spkd->skqd",
            weights.astype(jnp.bfloat16),
            chunk_cache[:, :, 1],
            preferred_element_type=jnp.float32,
        ) + jnp.einsum(
            "skqj,sjkd->skqd",
            fresh_weights.astype(jnp.bfloat16),
            chunk_fresh[:, :, 1],
            preferred_element_type=jnp.float32,
        )
        page_den = jnp.sum(weights, axis=-1) + jnp.sum(fresh_weights, axis=-1)
        slot_num = to_tokens(page_num).reshape(chunk_pages, NEW_TOKENS, device_count, owner_cols)
        slot_den = to_tokens(page_den[..., None]).reshape(chunk_pages, NEW_TOKENS, head_count)
        slot_peak = to_tokens(page_peak[..., None]).reshape(chunk_pages, NEW_TOKENS, head_count)
        packed = jnp.concatenate(
            [
                part.transpose(2, 0, 1, 3).reshape(device_count, chunk_pages, -1)
                for part in (slot_num, slot_den[:, :, head_pick], slot_peak[:, :, head_pick])
            ],
            axis=2,
        )
        return lax.all_to_all(packed, "blk", 0, 0, tiled=True)

    half_pages = request_page_count // 2
    arrived = jnp.concatenate(
        [page_exchange(0, half_pages), page_exchange(half_pages, request_page_count - half_pages)],
        axis=1,
    ).reshape(group_pages, -1)
    num_width = NEW_TOKENS * owner_cols
    head_width = NEW_TOKENS * owner_heads
    arrived_num = arrived[:, :num_width]
    arrived_den = arrived[:, num_width : num_width + head_width]
    arrived_peak = arrived[:, num_width + head_width :]
    top_flat = jnp.max(
        jnp.where(owner_of_page[:, None, :], arrived_peak.T[None], neg_large), axis=2
    )
    rescale = jnp.exp(arrived_peak - top_flat[page_of_req])
    rescaled = jnp.concatenate(
        [arrived_num * jnp.repeat(rescale, head_repeat, axis=1), arrived_den * rescale], axis=1
    )
    summed = jnp.einsum(
        "rp,px->rx", owner_of_page.astype(jnp.float32), rescaled, precision=lax.Precision.HIGHEST
    )
    num_own = summed[:, :num_width].reshape(request_count * NEW_TOKENS, owner_cols)
    den_own = summed[:, num_width:].reshape(request_count * NEW_TOKENS, owner_heads)
    attended_own = (num_own / jnp.repeat(den_own, head_repeat, axis=1)).astype(jnp.bfloat16)
    attended = lax.all_gather(attended_own, "blk", axis=1, tiled=True)
    return jnp.dot(attended, output_weight, preferred_element_type=jnp.float32).astype(jnp.bfloat16)


def solution(mesh):
    placed = (
        P("groups", "blk"),
        P(),
        P(None, "blk"),
        P(None, "blk"),
        P(None, "blk"),
        P("blk", None, None),
        P(None, None, "blk"),
        P(("groups", "blk"), None, None),
        P("groups"),
        P(),
        P("groups"),
        P("groups", None),
    )
    return jax.shard_map(
        local, mesh=mesh, in_specs=placed, out_specs=P("groups", "blk"), check_vma=False
    )
```

```python
import math

import jax
import jax.numpy as jnp
from jax import lax
from jax.experimental import pallas as pl
from jax.experimental.pallas import tpu as pltpu
from jax.sharding import PartitionSpec as P

QUERY_HEADS = 64
KEY_VALUE_HEADS = 8
HEAD_WIDTH = 128
PAGE_LENGTH = 128
NEW_TOKENS = 3


theta_base = 500000.0
neg_large = -1e30


def apply_rotation(values, token_positions, first_col, rot_limit):
    width_cols = values.shape[1]
    columns = first_col + jnp.arange(width_cols, dtype=jnp.int32)
    pair_index = (columns % HEAD_WIDTH // 2).astype(jnp.float32)
    inverse = jnp.exp(pair_index * (-2.0 * math.log(theta_base) / HEAD_WIDTH))
    angles = token_positions[:, None] * inverse[None, :]
    cos_val = jnp.cos(angles[:, 0::2])
    sine_val = jnp.sin(angles[:, 0::2])
    even_part = values[:, 0::2]
    odd_part = values[:, 1::2]
    turned = jnp.stack(
        [even_part * cos_val - odd_part * sine_val, even_part * sine_val + odd_part * cos_val],
        axis=-1,
    ).reshape(values.shape)
    return jnp.where((columns < rot_limit)[None, :], turned, values)


def rotation_kernel(values_ref, cos_ref, sine_ref, out_ref):
    values = values_ref[...]
    width = values.shape[1]
    following = pltpu.roll(values, width - 1, 1)
    preceding = pltpu.roll(values, 1, 1)
    even = lax.broadcasted_iota(jnp.int32, values.shape, 1) % 2 == 0
    cos_val = cos_ref[...]
    sine_val = sine_ref[...]
    out_ref[...] = jnp.where(
        even, values * cos_val - following * sine_val, preceding * sine_val + values * cos_val
    ).astype(out_ref.dtype)


def rotate_columns(values, token_positions, global_cols, rot_limit):
    pair_index = (global_cols % HEAD_WIDTH // 2).astype(jnp.float32)
    inverse = jnp.exp(pair_index * (-2.0 * math.log(theta_base) / HEAD_WIDTH))
    angles = token_positions[:, None] * inverse[None, :]
    rotated = (global_cols < rot_limit)[None, :]
    cos_val = jnp.where(rotated, jnp.cos(angles), 1.0)
    sine_val = jnp.where(rotated, jnp.sin(angles), 0.0)
    width = values.shape[1]
    pad = -(-width // 128) * 128 - width
    operands = [jnp.pad(a, ((0, 0), (0, pad))) for a in (values, cos_val, sine_val)]
    out = pl.pallas_call(
        rotation_kernel,
        out_shape=jax.ShapeDtypeStruct(operands[0].shape, jnp.bfloat16),
    )(*operands)
    return out[:, :width]


def normalize(layer_input_tokens, input_norm_gain):
    values = layer_input_tokens.astype(jnp.float32)
    mean_square = jnp.mean(values * values, axis=-1, keepdims=True)
    return (values * lax.rsqrt(mean_square + 1e-05) * input_norm_gain[None, :]).astype(jnp.bfloat16)


def positions_of(cached_lengths):
    steps_row = jnp.arange(NEW_TOKENS, dtype=jnp.int32)
    return (
        jnp.repeat(cached_lengths, NEW_TOKENS) + jnp.tile(steps_row, cached_lengths.shape[0])
    ).astype(jnp.float32)


def to_tokens(request_first_layout):
    request_count = request_first_layout.shape[0]
    trailing_shape = request_first_layout.shape[3:]
    query_group_width = QUERY_HEADS // KEY_VALUE_HEADS
    split_head_shape = request_first_layout.reshape(
        (request_count, KEY_VALUE_HEADS, NEW_TOKENS, query_group_width) + trailing_shape
    )
    order_axes = (0, 2, 1, 3) + tuple(range(4, 4 + len(trailing_shape)))
    return split_head_shape.transpose(order_axes).reshape(request_count * NEW_TOKENS, -1)


def butterfly(value, combine):
    size = lax.axis_size("blk")
    step = 1
    while step < size:
        masks = [step] if step * 2 >= size else [step, step * 2, step * 3]
        arrived = [lax.ppermute(value, "blk", [(i, i ^ m) for i in range(size)]) for m in masks]
        for other in arrived:
            value = combine(value, other)
        step *= 2 ** len(masks[:2])
    return value


def local(
    layer_input_tokens,
    input_norm_gain,
    query_weight,
    key_value_weight,
    output_weight,
    adapter_down_weight,
    adapter_up_weight,
    key_value_page_pool,
    request_adapter,
    adapter_storage_slot,
    cached_lengths,
    request_page_tables,
):
    own_index = lax.axis_index("blk")
    gathered = lax.all_gather(layer_input_tokens, "blk", axis=1, tiled=True)
    normalized_input = normalize(gathered, input_norm_gain)
    request_count = cached_lengths.shape[0]
    adapter_total = adapter_storage_slot.shape[0]
    choose = request_adapter[:, None] == jnp.arange(adapter_total, dtype=jnp.int32)[None, :]
    req_slot = jnp.sum(jnp.where(choose, adapter_storage_slot[None, :], 0), axis=1)
    token_cache_slot = jnp.repeat(req_slot, NEW_TOKENS)
    local_token_count = adapter_down_weight.shape[0]
    local_pick = (
        token_cache_slot[:, None] - own_index * local_token_count
        == jnp.arange(local_token_count, dtype=jnp.int32)[None, :]
    )
    output_projected = jnp.einsum(
        "ly,mxy->lmx", normalized_input, adapter_down_weight, preferred_element_type=jnp.float32
    )
    partial_codes = jnp.sum(jnp.where(local_pick[:, :, None], output_projected, 0.0), axis=1)
    adapter_choice_index = butterfly(partial_codes.astype(jnp.bfloat16), jnp.add)
    slot_count, adapter_rank, _ = adapter_up_weight.shape
    slot_pick = token_cache_slot[:, None] == jnp.arange(slot_count, dtype=jnp.int32)[None, :]
    spread_codes = jnp.where(
        slot_pick[:, :, None], adapter_choice_index[:, None, :], jnp.zeros((), jnp.bfloat16)
    ).reshape(token_cache_slot.shape[0], slot_count * adapter_rank)
    adapter_query_update = jnp.dot(
        spread_codes,
        adapter_up_weight.reshape(slot_count * adapter_rank, -1),
        preferred_element_type=jnp.float32,
    )
    token_positions = positions_of(cached_lengths)
    query_cols = query_weight.shape[1]
    keyval_cols = key_value_weight.shape[1]
    both_parts = jnp.concatenate(
        [
            jnp.dot(normalized_input, query_weight, preferred_element_type=jnp.float32)
            + adapter_query_update,
            jnp.dot(normalized_input, key_value_weight, preferred_element_type=jnp.float32),
        ],
        axis=1,
    )
    global_cols = jnp.concatenate(
        [
            own_index * query_cols + jnp.arange(query_cols, dtype=jnp.int32),
            own_index * keyval_cols + jnp.arange(keyval_cols, dtype=jnp.int32),
        ]
    )
    limits = jnp.concatenate(
        [
            jnp.full((query_cols,), QUERY_HEADS * HEAD_WIDTH, jnp.int32),
            jnp.full((keyval_cols,), KEY_VALUE_HEADS * HEAD_WIDTH, jnp.int32),
        ]
    )
    rotated_parts = rotate_columns(both_parts, token_positions, global_cols, limits)
    device_count = lax.axis_size("blk")
    request_page_count = key_value_page_pool.shape[0]
    table_width = request_page_tables.shape[1]
    group_pages = device_count * request_page_count
    listed_pages = request_page_tables.reshape(-1)
    listed_target = jnp.where(listed_pages >= 0, listed_pages, group_pages)
    page_of_req = (
        jnp.zeros((group_pages,), jnp.int32)
        .at[listed_target]
        .set(jnp.repeat(jnp.arange(request_count, dtype=jnp.int32), table_width), mode="drop")
    )
    page_used = jnp.zeros((group_pages,), jnp.bool_).at[listed_target].set(True, mode="drop")
    owner_of_page = (
        jnp.arange(request_count, dtype=jnp.int32)[:, None] == page_of_req[None, :]
    ) & page_used[None, :]
    part_rows = rotated_parts.reshape(request_count, NEW_TOKENS, -1)
    part_width = part_rows.shape[2]
    outgoing = part_rows[page_of_req].reshape(
        device_count, request_page_count, NEW_TOKENS * part_width
    )
    incoming = (
        lax.all_to_all(outgoing, "blk", 0, 0, tiled=True)
        .reshape(device_count, request_page_count, NEW_TOKENS, part_width)
        .transpose(1, 2, 0, 3)
    )
    slot_queries = incoming[..., :query_cols].reshape(request_page_count, NEW_TOKENS, -1)
    slot_fresh = incoming[..., query_cols:].reshape(
        request_page_count, NEW_TOKENS, 2, KEY_VALUE_HEADS, HEAD_WIDTH
    )
    query_group_width = QUERY_HEADS // KEY_VALUE_HEADS
    query_feature_width = query_group_width * NEW_TOKENS
    score_scale = 1.0 / math.sqrt(HEAD_WIDTH)
    page_ids = own_index * request_page_count + jnp.arange(request_page_count, dtype=jnp.int32)
    matches = request_page_tables[None, :, :] == page_ids[:, None, None]
    page_owner = jnp.any(matches, axis=2)
    page_live = jnp.any(page_owner, axis=1)
    page_slot = jnp.sum(
        jnp.where(matches, jnp.arange(table_width, dtype=jnp.int32)[None, None, :], 0), axis=(1, 2)
    )
    page_len = jnp.sum(jnp.where(page_owner, cached_lengths[None, :], 0), axis=1)
    key_pos = page_slot[:, None] * PAGE_LENGTH + jnp.arange(PAGE_LENGTH, dtype=jnp.int32)[None, :]
    key_valid = page_live[:, None] & (key_pos < page_len[:, None])
    valid_full = key_valid[:, None, None, :]
    takes_fresh = page_live & (page_slot == 0)
    step_of = jnp.arange(query_feature_width, dtype=jnp.int32) // query_group_width
    fresh_valid = takes_fresh[:, None, None, None] & (
        jnp.arange(NEW_TOKENS, dtype=jnp.int32)[None, None, None, :] <= step_of[None, None, :, None]
    )
    cache_pages = key_value_page_pool.reshape(
        request_page_count, PAGE_LENGTH, 2, KEY_VALUE_HEADS, HEAD_WIDTH
    )
    head_count = QUERY_HEADS
    owner_cols = query_cols
    owner_heads = max(1, owner_cols // HEAD_WIDTH)
    head_repeat = min(owner_cols, HEAD_WIDTH)
    owner_first_head = [(o * owner_cols) // HEAD_WIDTH for o in range(device_count)]
    head_pick = jnp.asarray(
        [[first + j for j in range(owner_heads)] for first in owner_first_head], jnp.int32
    )

    def page_exchange(first, chunk_pages):
        chunk_queries = slot_queries[first : first + chunk_pages]
        chunk_cache = cache_pages[first : first + chunk_pages]
        chunk_fresh = slot_fresh[first : first + chunk_pages]
        chunk_valid = valid_full[first : first + chunk_pages]
        chunk_fresh_valid = fresh_valid[first : first + chunk_pages]
        query_page = (
            chunk_queries.reshape(
                chunk_pages, NEW_TOKENS, KEY_VALUE_HEADS, query_group_width, HEAD_WIDTH
            )
            .transpose(0, 2, 1, 3, 4)
            .reshape(chunk_pages, KEY_VALUE_HEADS, query_feature_width, HEAD_WIDTH)
        )
        scores = (
            jnp.einsum(
                "skqd,spkd->skqp", query_page, chunk_cache[:, :, 0], preferred_element_type=jnp.float32
            )
            * score_scale
        )
        fresh_scores = (
            jnp.einsum(
                "skqd,sjkd->skqj", query_page, chunk_fresh[:, :, 0], preferred_element_type=jnp.float32
            )
            * score_scale
        )
        masked = jnp.where(chunk_valid, scores, neg_large)
        fresh_masked = jnp.where(chunk_fresh_valid, fresh_scores, neg_large)
        page_peak = jnp.maximum(jnp.max(masked, axis=-1), jnp.max(fresh_masked, axis=-1))
        weights = jnp.where(chunk_valid, jnp.exp(masked - page_peak[..., None]), 0.0)
        fresh_weights = jnp.where(chunk_fresh_valid, jnp.exp(fresh_masked - page_peak[..., None]), 0.0)
        page_num = jnp.einsum(
            "skqp,spkd->skqd",
            weights.astype(jnp.bfloat16),
            chunk_cache[:, :, 1],
            preferred_element_type=jnp.float32,
        ) + jnp.einsum(
            "skqj,sjkd->skqd",
            fresh_weights.astype(jnp.bfloat16),
            chunk_fresh[:, :, 1],
            preferred_element_type=jnp.float32,
        )
        page_den = jnp.sum(weights, axis=-1) + jnp.sum(fresh_weights, axis=-1)
        slot_num = to_tokens(page_num).reshape(chunk_pages, NEW_TOKENS, device_count, owner_cols)
        slot_den = to_tokens(page_den[..., None]).reshape(chunk_pages, NEW_TOKENS, head_count)
        slot_peak = to_tokens(page_peak[..., None]).reshape(chunk_pages, NEW_TOKENS, head_count)
        packed = jnp.concatenate(
            [
                part.transpose(2, 0, 1, 3).reshape(device_count, chunk_pages, -1)
                for part in (slot_num, slot_den[:, :, head_pick], slot_peak[:, :, head_pick])
            ],
            axis=2,
        )
        return lax.all_to_all(packed, "blk", 0, 0, tiled=True)

    half_pages = (3 * request_page_count) // 8
    arrived = jnp.concatenate(
        [page_exchange(0, half_pages), page_exchange(half_pages, request_page_count - half_pages)],
        axis=1,
    ).reshape(group_pages, -1)
    num_width = NEW_TOKENS * owner_cols
    head_width = NEW_TOKENS * owner_heads
    arrived_num = arrived[:, :num_width]
    arrived_den = arrived[:, num_width : num_width + head_width]
    arrived_peak = arrived[:, num_width + head_width :]
    top_flat = jnp.max(
        jnp.where(owner_of_page[:, None, :], arrived_peak.T[None], neg_large), axis=2
    )
    rescale = jnp.exp(arrived_peak - top_flat[page_of_req])
    rescaled = jnp.concatenate(
        [arrived_num * jnp.repeat(rescale, head_repeat, axis=1), arrived_den * rescale], axis=1
    )
    summed = jnp.einsum(
        "rp,px->rx", owner_of_page.astype(jnp.float32), rescaled, precision=lax.Precision.HIGHEST
    )
    num_own = summed[:, :num_width].reshape(request_count * NEW_TOKENS, owner_cols)
    den_own = summed[:, num_width:].reshape(request_count * NEW_TOKENS, owner_heads)
    attended_own = (num_own / jnp.repeat(den_own, head_repeat, axis=1)).astype(jnp.bfloat16)
    attended = lax.all_gather(attended_own, "blk", axis=1, tiled=True)
    return jnp.dot(attended, output_weight, preferred_element_type=jnp.float32).astype(jnp.bfloat16)


def solution(mesh):
    placed = (
        P("groups", "blk"),
        P(),
        P(None, "blk"),
        P(None, "blk"),
        P(None, "blk"),
        P("blk", None, None),
        P(None, None, "blk"),
        P(("groups", "blk"), None, None),
        P("groups"),
        P(),
        P("groups"),
        P("groups", None),
    )
    return jax.shard_map(
        local, mesh=mesh, in_specs=placed, out_specs=P("groups", "blk"), check_vma=False
    )
```
